256 devices in a mesh: group: 8 (over z_hi, core), slab: 32 (over z_lo, y, x).
Axes of the slice: x: 4, y: 4, z: 8 (z_hi: 4, z_lo: 2; z = z_hi * 2 + z_lo), core: 2. Of those that a mesh axis runs over, the one named last changes fastest.
Arguments:
- volume: float32 [8, 1024, 256], P('group', 'slab'), may hold values from -6 to 6
- consensus: float32 [1024, 256], P('slab'), may hold values from -6 to 6
- scaled_dual: float32 [8, 1024, 256], P('group', 'slab'), may hold values from -3 to 3
- amplitude: float32 [8, 4, 1024, 1024], P('group', None, 'slab'), may hold values from 0.5 to 2
- fresnel: float32 [4], replicated, may hold values from 0.05 to 0.5
- ray_index: int32 [8, 8, 1024], P('group'), may hold values from 0 to 255
- ray_weight: float32 [8, 8, 1024], P('group'), may hold values from 0.05 to 0.3
Outputs:
- volume_next: float32 [8, 1024, 256], P('group', 'slab')
- consensus_next: float32 [1024, 256], P('slab')
- dual_next: float32 [8, 1024, 256], P('group', 'slab')
The draws below stay inside these ranges and needn't reach their ends.
Inputs may be any that keep to these rules, and one draw needn't show every extreme that they name: `ray_index`: taps of one column may name the same cell.
All inputs are finite; a program needn't handle non-finite values.
Results may differ from the reference program's by a relative error of at most 0.0003.
Values sent between devices are 32-bit elements; how exact they have to be, the bound alone decides.
No kernel may reach another device: no remote copies, remote signals or barrier semaphores. Data moves between devices by JAX's collectives and lax.ppermute only.
A program may use at most 64 MiB of HBM per device.

```python
import math
import jax
import jax.numpy as jnp
from jax import lax

HOLOGRAM = 1024
DISTANCES = 4
RAY_TAPS = 8
SLICE_CELLS = 256
GROUP_COUNT = 8


def set_ends(entries, key, low, largest):
    shape = entries.shape
    place = [jax.random.randint(jax.random.fold_in(key, axis), (), 0, shape[axis]) for axis in range(len(shape))]
    entries = entries.at[tuple(place)].set(low)
    longest = shape.index(max(shape))
    place[longest] = (place[longest] + 1) % shape[longest]
    return entries.at[tuple(place)].set(largest)


def steps_of(rng, dims, shards, low, largest):
    def one(axis_at, shards_of):
        heights = jax.random.uniform(jax.random.fold_in(jax.random.fold_in(rng, 6), axis_at), (shards_of,), jnp.float32, low / len(shards), largest / len(shards))
        return jnp.repeat(jnp.exp(heights), dims[axis_at] // shards_of).reshape((-1,) + (1,) * (len(dims) - axis_at - 1))

    loudness = one(*shards[0])
    for cut in shards[1:]:
        loudness = loudness * one(*cut)
    return loudness


def noise(own_key, shape, scale, limit, cuts=(), kind=jnp.bfloat16):
    result = scale * jax.random.normal(own_key, shape, jnp.float32)
    if cuts:
        result = result * steps_of(own_key, shape, cuts, -0.22, 0.18)
    return jnp.clip(result, -limit, limit).astype(kind)


def setup_inputs(seed: int = 0) -> dict:
    streams_of = jax.random.split(jax.random.key(seed), 8)
    volume = noise(streams_of[0], (GROUP_COUNT, HOLOGRAM, SLICE_CELLS), 1.0, 6.0, ((0, 8), (1, 32)), jnp.float32)
    consensus = noise(streams_of[1], (HOLOGRAM, SLICE_CELLS), 1.0, 6.0, ((0, 32),), jnp.float32)
    scaled_dual = noise(streams_of[2], (GROUP_COUNT, HOLOGRAM, SLICE_CELLS), 0.5, 3.0, ((0, 8), (1, 32)), jnp.float32)
    amplitude = jnp.clip(jnp.exp(math.log(2.0) - 1.3862944 * jax.random.uniform(streams_of[3], (GROUP_COUNT, DISTANCES, HOLOGRAM, HOLOGRAM), jnp.float32) ** steps_of(streams_of[3], (GROUP_COUNT, DISTANCES, HOLOGRAM, HOLOGRAM), ((0, 8), (2, 32)), -0.2, 0.2)), 0.5, 2.0)
    fresnel = jnp.clip(jnp.exp(jax.random.uniform(streams_of[4], (DISTANCES,), jnp.float32, math.log(0.05), math.log(0.5))), 0.05, 0.5)
    ray_index = set_ends(jax.random.randint(streams_of[5], (GROUP_COUNT, RAY_TAPS, HOLOGRAM), 0, SLICE_CELLS), jax.random.fold_in(streams_of[5], 1), 0, SLICE_CELLS - 1).astype(jnp.int32)
    ray_weight = jnp.clip(0.05 + 0.25 * jax.random.uniform(streams_of[6], (GROUP_COUNT, RAY_TAPS, HOLOGRAM), jnp.float32) ** steps_of(streams_of[6], (GROUP_COUNT, RAY_TAPS, HOLOGRAM), ((0, 8),), -0.2, 0.2), 0.05, 0.3)
    return dict(volume=volume, consensus=consensus, scaled_dual=scaled_dual, amplitude=amplitude, fresnel=fresnel, ray_index=ray_index, ray_weight=ray_weight)


step_size = 0.5
penalty = 0.5
mod_floor = 0.25

def build_projector(indices, weights):
    cell_ids = jnp.arange(SLICE_CELLS, dtype=jnp.int32)
    projector = jnp.zeros((HOLOGRAM, SLICE_CELLS), weights.dtype)
    for tap_number in range(RAY_TAPS):
        hit = (indices[tap_number][:, None] == cell_ids[None, :]).astype(weights.dtype)
        projector = projector + weights[tap_number][:, None] * hit
    return projector

def make_kernel(fresnel):
    frequency = jnp.arange(HOLOGRAM, dtype=jnp.int32)
    centered = jnp.where(frequency < HOLOGRAM // 2, frequency, frequency - HOLOGRAM)
    radius = (centered[:, None] * centered[:, None] + centered[None, :] * centered[None, :]).astype(fresnel.dtype)
    phase = -math.pi * fresnel[:, None, None] * radius[None] / HOLOGRAM
    return lax.complex(jnp.cos(phase), jnp.sin(phase))

def reference(volume, consensus, scaled_dual, amplitude, fresnel, ray_index, ray_weight):
    kernel = make_kernel(fresnel)

    def one_group(packed):
        volume_g, dual_g, amplitude_g, index_g, weight_g = packed
        projector = build_projector(index_g, weight_g)
        thickness = jnp.dot(volume_g, projector.T, precision=lax.Precision.HIGHEST)
        wavefront = lax.complex(jnp.cos(thickness), jnp.sin(thickness))
        spectrum = jnp.fft.fft2(wavefront)
        total = jnp.zeros_like(spectrum)
        for distance in range(DISTANCES):
            field = jnp.fft.ifft2(kernel[distance] * spectrum)
            magnitude = jnp.sqrt(field.real * field.real + field.imag * field.imag)
            moduli = field * (amplitude_g[distance] / jnp.maximum(magnitude, mod_floor))
            total = total + jnp.conj(kernel[distance]) * jnp.fft.fft2(moduli)
        back = jnp.fft.ifft2(total / DISTANCES)
        gradient = jnp.cos(thickness) * back.imag - jnp.sin(thickness) * back.real
        bprojected = jnp.dot(gradient, projector, precision=lax.Precision.HIGHEST)
        return volume_g + step_size * (bprojected - penalty * (volume_g - consensus + dual_g))
    volume_next = lax.map(one_group, (volume, scaled_dual, amplitude, ray_index, ray_weight))
    consensus_next = lax.optimization_barrier(jnp.sum(volume_next + scaled_dual, axis=0)) / GROUP_COUNT
    dual_next = scaled_dual + volume_next - consensus_next[None]
    return (volume_next, consensus_next, dual_next)
```

```python
import math

import jax
import jax.numpy as jnp
from jax import lax
from jax.sharding import PartitionSpec as P

HOLOGRAM = 1024
DISTANCES = 4


step_size = 0.5
penalty = 0.5
mod_floor = 0.25
highest = lax.Precision.HIGHEST


def dft_tables(count):
    index = jnp.arange(count, dtype=jnp.int32)
    angle = 2.0 * math.pi / count * (index[:, None] * index[None, :] % count).astype(jnp.float32)
    return (jnp.cos(angle), jnp.sin(angle))


def complex_contract(real_part, imag_part, tables, form, inverse):
    cos_table, sin_table = tables
    real_cos = jnp.einsum(form, real_part, cos_table, precision=highest)
    real_sin = jnp.einsum(form, real_part, sin_table, precision=highest)
    imag_cos = jnp.einsum(form, imag_part, cos_table, precision=highest)
    imag_sin = jnp.einsum(form, imag_part, sin_table, precision=highest)
    if inverse:
        return (real_cos - imag_sin, imag_cos + real_sin)
    return (real_cos + imag_sin, imag_cos - real_sin)


def twiddle_apply(real_part, imag_part, twiddle, inverse):
    twiddle_cos, twiddle_sin = twiddle
    if inverse:
        return (
            real_part * twiddle_cos - imag_part * twiddle_sin,
            imag_part * twiddle_cos + real_part * twiddle_sin,
        )
    return (
        real_part * twiddle_cos + imag_part * twiddle_sin,
        imag_part * twiddle_cos - real_part * twiddle_sin,
    )


def along_last(values, plan, inverse):
    outer_tables, inner_tables, twiddle = plan
    outer_len = outer_tables[0].shape[0]
    inner_len = inner_tables[0].shape[0]
    real_part = values[..., 0, :, :]
    imag_part = values[..., 1, :, :]
    shape = real_part.shape
    length = shape[-1]
    real_part = real_part.reshape(shape[:-1] + (outer_len, inner_len))
    imag_part = imag_part.reshape(shape[:-1] + (outer_len, inner_len))
    outer_form = "...ab,ak->...kb"
    inner_form = "...ab,bl->...al"
    if inverse:
        real_part, imag_part = complex_contract(
            real_part, imag_part, inner_tables, inner_form, True
        )
        real_part, imag_part = twiddle_apply(real_part, imag_part, twiddle, True)
        real_part, imag_part = complex_contract(
            real_part, imag_part, outer_tables, outer_form, True
        )
    else:
        real_part, imag_part = complex_contract(
            real_part, imag_part, outer_tables, outer_form, False
        )
        real_part, imag_part = twiddle_apply(real_part, imag_part, twiddle, False)
        real_part, imag_part = complex_contract(
            real_part, imag_part, inner_tables, inner_form, False
        )
    result = jnp.stack([real_part.reshape(shape), imag_part.reshape(shape)], axis=-3)
    if inverse:
        return result * (1.0 / length)
    return result


def along_first(values, plan, inverse):
    outer_tables, inner_tables, twiddle = plan
    outer_len = outer_tables[0].shape[0]
    inner_len = inner_tables[0].shape[0]
    real_part = values[..., 0, :, :]
    imag_part = values[..., 1, :, :]
    shape = real_part.shape
    length = shape[-2]
    split_shape = shape[:-2] + (outer_len, inner_len, shape[-1])
    real_part = real_part.reshape(split_shape)
    imag_part = imag_part.reshape(split_shape)
    twiddle_cols = (twiddle[0][:, :, None], twiddle[1][:, :, None])
    outer_form = "...abw,ak->...kbw"
    inner_form = "...abw,bl->...alw"
    if inverse:
        real_part, imag_part = complex_contract(
            real_part, imag_part, inner_tables, inner_form, True
        )
        real_part, imag_part = twiddle_apply(real_part, imag_part, twiddle_cols, True)
        real_part, imag_part = complex_contract(
            real_part, imag_part, outer_tables, outer_form, True
        )
    else:
        real_part, imag_part = complex_contract(
            real_part, imag_part, outer_tables, outer_form, False
        )
        real_part, imag_part = twiddle_apply(real_part, imag_part, twiddle_cols, False)
        real_part, imag_part = complex_contract(
            real_part, imag_part, inner_tables, inner_form, False
        )
    result = jnp.stack([real_part.reshape(shape), imag_part.reshape(shape)], axis=-3)
    if inverse:
        return result * (1.0 / length)
    return result


def shards(volume, consensus, scaled_dual, amplitude, fresnel, ray_index, ray_weight):
    slice_cells = volume.shape[2]
    length = amplitude.shape[3]
    slabs = lax.axis_size("slab")
    width = length // slabs
    groups = lax.axis_size("group")
    inner_len = min(128, length)
    outer_len = length // inner_len
    outer_index = jnp.arange(outer_len, dtype=jnp.int32)
    inner_index = jnp.arange(inner_len, dtype=jnp.int32)
    twiddle_angle = (
        2.0 * math.pi / length * (outer_index[:, None] * inner_index[None, :]).astype(jnp.float32)
    )
    plan = (
        dft_tables(outer_len),
        dft_tables(inner_len),
        (jnp.cos(twiddle_angle), jnp.sin(twiddle_angle)),
    )
    cell_ids = jnp.arange(slice_cells, dtype=jnp.int32)
    projector = jnp.zeros((length, slice_cells), jnp.float32)
    for tap_number in range(ray_index.shape[1]):
        hit = (ray_index[0, tap_number][:, None] == cell_ids[None, :]).astype(jnp.float32)
        projector = projector + ray_weight[0, tap_number][:, None] * hit
    thickness = lax.dot_general(volume[0], projector, (((1,), (1,)), ((), ())), precision=highest)
    wavefront = jnp.stack([jnp.cos(thickness), jnp.sin(thickness)])
    row_spectrum = along_last(wavefront, plan, False)
    spectrum = along_first(
        lax.all_to_all(row_spectrum, "slab", split_axis=2, concat_axis=1, tiled=True), plan, False
    )
    position = jnp.arange(length, dtype=jnp.int32)
    row_freq = position // inner_len + outer_len * (position % inner_len)
    column_pos = lax.axis_index("slab") * width + jnp.arange(width, dtype=jnp.int32)
    column_freq = column_pos // inner_len + outer_len * (column_pos % inner_len)
    centered_rows = jnp.where(row_freq < length // 2, row_freq, row_freq - length)
    centered_cols = jnp.where(column_freq < length // 2, column_freq, column_freq - length)
    radius = (
        centered_rows[:, None] * centered_rows[:, None]
        + centered_cols[None, :] * centered_cols[None, :]
    ).astype(jnp.float32)
    phase = -math.pi * fresnel[:, None, None] * radius[None] / HOLOGRAM
    kernel_real = jnp.cos(phase)
    kernel_imag = jnp.sin(phase)
    propagated = jnp.stack(
        [
            kernel_real * spectrum[0] - kernel_imag * spectrum[1],
            kernel_real * spectrum[1] + kernel_imag * spectrum[0],
        ],
        axis=1,
    )
    column_fields = along_first(propagated, plan, True)

    def rows_inverse(values):
        return along_last(values, plan, True)

    def columns_forward(values):
        return along_first(values, plan, False)

    fields = rows_inverse(
        lax.all_to_all(column_fields, "slab", split_axis=2, concat_axis=3, tiled=True)
    )
    magnitude = jnp.sqrt(fields[:, 0] * fields[:, 0] + fields[:, 1] * fields[:, 1])
    factor = amplitude[0] / jnp.maximum(magnitude, mod_floor)
    moduli_rows = along_last(fields * factor[:, None], plan, False)
    moduli_spectra = columns_forward(
        lax.all_to_all(moduli_rows, "slab", split_axis=3, concat_axis=2, tiled=True)
    )
    total_real = jnp.sum(
        kernel_real * moduli_spectra[:, 0] + kernel_imag * moduli_spectra[:, 1], axis=0
    )
    total_imag = jnp.sum(
        kernel_real * moduli_spectra[:, 1] - kernel_imag * moduli_spectra[:, 0], axis=0
    )
    averaged = jnp.stack([total_real, total_imag]) / DISTANCES
    column_back = along_first(averaged, plan, True)
    back = rows_inverse(
        lax.all_to_all(column_back, "slab", split_axis=1, concat_axis=2, tiled=True)
    )
    gradient = jnp.cos(thickness) * back[1] - jnp.sin(thickness) * back[0]
    bprojected = jnp.matmul(gradient, projector, precision=highest)
    volume_next = volume[0] + step_size * (
        bprojected - penalty * (volume[0] - consensus + scaled_dual[0])
    )
    combined = volume_next + scaled_dual[0]
    consensus_next = lax.psum(combined, "group") / groups
    dual_next = scaled_dual[0] + volume_next - consensus_next
    return (volume_next[None], consensus_next, dual_next[None])


def solution(mesh):
    placed = (
        P("group", "slab", None),
        P("slab", None),
        P("group", "slab", None),
        P("group", None, "slab", None),
        P(),
        P("group", None, None),
        P("group", None, None),
    )
    return jax.shard_map(
        shards,
        mesh=mesh,
        in_specs=placed,
        out_specs=(P("group", "slab", None), P("slab", None), P("group", "slab", None)),
        check_vma=False,
    )
```

```python
import math

import jax
import jax.numpy as jnp
from jax import lax
from jax.sharding import PartitionSpec as P

HOLOGRAM = 1024
DISTANCES = 4


step_size = 0.5
penalty = 0.5
mod_floor = 0.25
highest = lax.Precision.HIGHEST


def dft_tables(count):
    index = jnp.arange(count, dtype=jnp.int32)
    angle = 2.0 * math.pi / count * (index[:, None] * index[None, :] % count).astype(jnp.float32)
    return (jnp.cos(angle), jnp.sin(angle))


def complex_contract(real_part, imag_part, tables, form, inverse):
    cos_table, sin_table = tables
    real_cos = jnp.einsum(form, real_part, cos_table, precision=highest)
    real_sin = jnp.einsum(form, real_part, sin_table, precision=highest)
    imag_cos = jnp.einsum(form, imag_part, cos_table, precision=highest)
    imag_sin = jnp.einsum(form, imag_part, sin_table, precision=highest)
    if inverse:
        return (real_cos - imag_sin, imag_cos + real_sin)
    return (real_cos + imag_sin, imag_cos - real_sin)


def twiddle_apply(real_part, imag_part, twiddle, inverse):
    twiddle_cos, twiddle_sin = twiddle
    if inverse:
        return (
            real_part * twiddle_cos - imag_part * twiddle_sin,
            imag_part * twiddle_cos + real_part * twiddle_sin,
        )
    return (
        real_part * twiddle_cos + imag_part * twiddle_sin,
        imag_part * twiddle_cos - real_part * twiddle_sin,
    )


def along_last(values, plan, inverse):
    outer_tables, inner_tables, twiddle = plan
    outer_len = outer_tables[0].shape[0]
    inner_len = inner_tables[0].shape[0]
    real_part = values[..., 0, :, :]
    imag_part = values[..., 1, :, :]
    shape = real_part.shape
    length = shape[-1]
    real_part = real_part.reshape(shape[:-1] + (outer_len, inner_len))
    imag_part = imag_part.reshape(shape[:-1] + (outer_len, inner_len))
    outer_form = "...ab,ak->...kb"
    inner_form = "...ab,bl->...al"
    if inverse:
        real_part, imag_part = complex_contract(
            real_part, imag_part, inner_tables, inner_form, True
        )
        real_part, imag_part = twiddle_apply(real_part, imag_part, twiddle, True)
        real_part, imag_part = complex_contract(
            real_part, imag_part, outer_tables, outer_form, True
        )
    else:
        real_part, imag_part = complex_contract(
            real_part, imag_part, outer_tables, outer_form, False
        )
        real_part, imag_part = twiddle_apply(real_part, imag_part, twiddle, False)
        real_part, imag_part = complex_contract(
            real_part, imag_part, inner_tables, inner_form, False
        )
    result = jnp.stack([real_part.reshape(shape), imag_part.reshape(shape)], axis=-3)
    if inverse:
        return result * (1.0 / length)
    return result


def along_first(values, plan, inverse):
    outer_tables, inner_tables, twiddle = plan
    outer_len = outer_tables[0].shape[0]
    inner_len = inner_tables[0].shape[0]
    real_part = values[..., 0, :, :]
    imag_part = values[..., 1, :, :]
    shape = real_part.shape
    length = shape[-2]
    split_shape = shape[:-2] + (outer_len, inner_len, shape[-1])
    real_part = real_part.reshape(split_shape)
    imag_part = imag_part.reshape(split_shape)
    twiddle_cols = (twiddle[0][:, :, None], twiddle[1][:, :, None])
    outer_form = "...abw,ak->...kbw"
    inner_form = "...abw,bl->...alw"
    if inverse:
        real_part, imag_part = complex_contract(
            real_part, imag_part, inner_tables, inner_form, True
        )
        real_part, imag_part = twiddle_apply(real_part, imag_part, twiddle_cols, True)
        real_part, imag_part = complex_contract(
            real_part, imag_part, outer_tables, outer_form, True
        )
    else:
        real_part, imag_part = complex_contract(
            real_part, imag_part, outer_tables, outer_form, False
        )
        real_part, imag_part = twiddle_apply(real_part, imag_part, twiddle_cols, False)
        real_part, imag_part = complex_contract(
            real_part, imag_part, inner_tables, inner_form, False
        )
    result = jnp.stack([real_part.reshape(shape), imag_part.reshape(shape)], axis=-3)
    if inverse:
        return result * (1.0 / length)
    return result


def shards(volume, consensus, scaled_dual, amplitude, fresnel, ray_index, ray_weight):
    slice_cells = volume.shape[2]
    length = amplitude.shape[3]
    slabs = lax.axis_size("slab")
    width = length // slabs
    groups = lax.axis_size("group")
    inner_len = min(128, length)
    outer_len = length // inner_len
    outer_index = jnp.arange(outer_len, dtype=jnp.int32)
    inner_index = jnp.arange(inner_len, dtype=jnp.int32)
    twiddle_angle = (
        2.0 * math.pi / length * (outer_index[:, None] * inner_index[None, :]).astype(jnp.float32)
    )
    plan = (
        dft_tables(outer_len),
        dft_tables(inner_len),
        (jnp.cos(twiddle_angle), jnp.sin(twiddle_angle)),
    )
    cell_ids = jnp.arange(slice_cells, dtype=jnp.int32)
    projector = jnp.zeros((length, slice_cells), jnp.float32)
    for tap_number in range(ray_index.shape[1]):
        hit = (ray_index[0, tap_number][:, None] == cell_ids[None, :]).astype(jnp.float32)
        projector = projector + ray_weight[0, tap_number][:, None] * hit
    thickness = lax.dot_general(volume[0], projector, (((1,), (1,)), ((), ())), precision=highest)
    wavefront = jnp.stack([jnp.cos(thickness), jnp.sin(thickness)])
    row_spectrum = along_last(wavefront, plan, False)
    spectrum = along_first(
        lax.all_to_all(row_spectrum, "slab", split_axis=2, concat_axis=1, tiled=True), plan, False
    )
    position = jnp.arange(length, dtype=jnp.int32)
    row_freq = position // inner_len + outer_len * (position % inner_len)
    column_pos = lax.axis_index("slab") * width + jnp.arange(width, dtype=jnp.int32)
    column_freq = column_pos // inner_len + outer_len * (column_pos % inner_len)
    centered_rows = jnp.where(row_freq < length // 2, row_freq, row_freq - length)
    centered_cols = jnp.where(column_freq < length // 2, column_freq, column_freq - length)
    radius = (
        centered_rows[:, None] * centered_rows[:, None]
        + centered_cols[None, :] * centered_cols[None, :]
    ).astype(jnp.float32)
    phase = -math.pi * fresnel[:, None, None] * radius[None] / HOLOGRAM
    kernel_real = jnp.cos(phase)
    kernel_imag = jnp.sin(phase)
    propagated = jnp.stack(
        [
            kernel_real * spectrum[0] - kernel_imag * spectrum[1],
            kernel_real * spectrum[1] + kernel_imag * spectrum[0],
        ],
        axis=1,
    )
    column_fields = along_first(propagated, plan, True)

    def rows_inverse(values):
        return along_last(values, plan, True)

    def columns_forward(values):
        return along_first(values, plan, False)

    fields = rows_inverse(
        lax.all_to_all(column_fields, "slab", split_axis=2, concat_axis=3, tiled=True)
    )
    magnitude = jnp.sqrt(fields[:, 0] * fields[:, 0] + fields[:, 1] * fields[:, 1])
    factor = amplitude[0] / jnp.maximum(magnitude, mod_floor)
    moduli_rows = along_last(fields * factor[:, None], plan, False)
    moduli_spectra = columns_forward(
        lax.all_to_all(moduli_rows, "slab", split_axis=3, concat_axis=2, tiled=True)
    )
    total_real = jnp.sum(
        kernel_real * moduli_spectra[:, 0] + kernel_imag * moduli_spectra[:, 1], axis=0
    )
    total_imag = jnp.sum(
        kernel_real * moduli_spectra[:, 1] - kernel_imag * moduli_spectra[:, 0], axis=0
    )
    averaged = jnp.stack([total_real, total_imag]) / DISTANCES
    column_back = along_first(averaged, plan, True)
    back = rows_inverse(
        lax.all_to_all(column_back, "slab", split_axis=1, concat_axis=2, tiled=True)
    )
    gradient = jnp.cos(thickness) * back[1] - jnp.sin(thickness) * back[0]
    bprojected = jnp.matmul(gradient, projector, precision=highest)
    volume_next = volume[0] + step_size * (
        bprojected - penalty * (volume[0] - consensus + scaled_dual[0])
    )
    combined = volume_next + scaled_dual[0]
    total = combined
    step = 1
    while step < groups:
        pairs = [(index, index ^ step) for index in range(groups)]
        total = total + lax.ppermute(total, "group", pairs)
        step *= 2
    consensus_next = total / groups
    dual_next = scaled_dual[0] + volume_next - consensus_next
    return (volume_next[None], consensus_next, dual_next[None])


def solution(mesh):
    placed = (
        P("group", "slab", None),
        P("slab", None),
        P("group", "slab", None),
        P("group", None, "slab", None),
        P(),
        P("group", None, None),
        P("group", None, None),
    )
    return jax.shard_map(
        shards,
        mesh=mesh,
        in_specs=placed,
        out_specs=(P("group", "slab", None), P("slab", None), P("group", "slab", None)),
        check_vma=False,
    )
```

```python
import math

import jax
import jax.numpy as jnp
from jax import lax
from jax.sharding import PartitionSpec as P

HOLOGRAM = 1024
DISTANCES = 4


step_size = 0.5
penalty = 0.5
mod_floor = 0.25
highest = lax.Precision.HIGHEST


def dft_tables(count):
    index = jnp.arange(count, dtype=jnp.int32)
    angle = 2.0 * math.pi / count * (index[:, None] * index[None, :] % count).astype(jnp.float32)
    return (jnp.cos(angle), jnp.sin(angle))


def complex_contract(real_part, imag_part, tables, form, inverse):
    cos_table, sin_table = tables
    real_cos = jnp.einsum(form, real_part, cos_table, precision=highest)
    real_sin = jnp.einsum(form, real_part, sin_table, precision=highest)
    imag_cos = jnp.einsum(form, imag_part, cos_table, precision=highest)
    imag_sin = jnp.einsum(form, imag_part, sin_table, precision=highest)
    if inverse:
        return (real_cos - imag_sin, imag_cos + real_sin)
    return (real_cos + imag_sin, imag_cos - real_sin)


def twiddle_apply(real_part, imag_part, twiddle, inverse):
    twiddle_cos, twiddle_sin = twiddle
    if inverse:
        return (
            real_part * twiddle_cos - imag_part * twiddle_sin,
            imag_part * twiddle_cos + real_part * twiddle_sin,
        )
    return (
        real_part * twiddle_cos + imag_part * twiddle_sin,
        imag_part * twiddle_cos - real_part * twiddle_sin,
    )


def along_last(values, plan, inverse):
    outer_tables, inner_tables, twiddle = plan
    outer_len = outer_tables[0].shape[0]
    inner_len = inner_tables[0].shape[0]
    real_part = values[..., 0, :, :]
    imag_part = values[..., 1, :, :]
    shape = real_part.shape
    length = shape[-1]
    real_part = real_part.reshape(shape[:-1] + (outer_len, inner_len))
    imag_part = imag_part.reshape(shape[:-1] + (outer_len, inner_len))
    outer_form = "...ab,ak->...kb"
    inner_form = "...ab,bl->...al"
    if inverse:
        real_part, imag_part = complex_contract(
            real_part, imag_part, inner_tables, inner_form, True
        )
        real_part, imag_part = twiddle_apply(real_part, imag_part, twiddle, True)
        real_part, imag_part = complex_contract(
            real_part, imag_part, outer_tables, outer_form, True
        )
    else:
        real_part, imag_part = complex_contract(
            real_part, imag_part, outer_tables, outer_form, False
        )
        real_part, imag_part = twiddle_apply(real_part, imag_part, twiddle, False)
        real_part, imag_part = complex_contract(
            real_part, imag_part, inner_tables, inner_form, False
        )
    result = jnp.stack([real_part.reshape(shape), imag_part.reshape(shape)], axis=-3)
    if inverse:
        return result * (1.0 / length)
    return result


def along_first(values, plan, inverse):
    outer_tables, inner_tables, twiddle = plan
    outer_len = outer_tables[0].shape[0]
    inner_len = inner_tables[0].shape[0]
    real_part = values[..., 0, :, :]
    imag_part = values[..., 1, :, :]
    shape = real_part.shape
    length = shape[-2]
    split_shape = shape[:-2] + (outer_len, inner_len, shape[-1])
    real_part = real_part.reshape(split_shape)
    imag_part = imag_part.reshape(split_shape)
    twiddle_cols = (twiddle[0][:, :, None], twiddle[1][:, :, None])
    outer_form = "...abw,ak->...kbw"
    inner_form = "...abw,bl->...alw"
    if inverse:
        real_part, imag_part = complex_contract(
            real_part, imag_part, inner_tables, inner_form, True
        )
        real_part, imag_part = twiddle_apply(real_part, imag_part, twiddle_cols, True)
        real_part, imag_part = complex_contract(
            real_part, imag_part, outer_tables, outer_form, True
        )
    else:
        real_part, imag_part = complex_contract(
            real_part, imag_part, outer_tables, outer_form, False
        )
        real_part, imag_part = twiddle_apply(real_part, imag_part, twiddle_cols, False)
        real_part, imag_part = complex_contract(
            real_part, imag_part, inner_tables, inner_form, False
        )
    result = jnp.stack([real_part.reshape(shape), imag_part.reshape(shape)], axis=-3)
    if inverse:
        return result * (1.0 / length)
    return result


def exchange(values, slabs, width):
    lead = values.shape[:-2]
    rank = len(lead)
    blocks = values.reshape(lead + (width, slabs, width))
    order = (rank + 1,) + tuple(range(rank)) + (rank, rank + 2)
    outgoing = jnp.transpose(blocks, order).reshape((slabs,) + lead + (width * width,))
    incoming = lax.all_to_all(outgoing, "slab", split_axis=0, concat_axis=0, tiled=True)
    incoming = incoming.reshape((slabs,) + lead + (width, width))
    order = tuple(range(1, rank + 1)) + (rank + 2, 0, rank + 1)
    return jnp.transpose(incoming, order).reshape(lead + (width, slabs * width))


def shards(volume, consensus, scaled_dual, amplitude, fresnel, ray_index, ray_weight):
    slice_cells = volume.shape[2]
    length = amplitude.shape[3]
    slabs = lax.axis_size("slab")
    width = length // slabs
    groups = lax.axis_size("group")
    inner_len = min(128, length)
    outer_len = length // inner_len
    outer_index = jnp.arange(outer_len, dtype=jnp.int32)
    inner_index = jnp.arange(inner_len, dtype=jnp.int32)
    twiddle_angle = (
        2.0 * math.pi / length * (outer_index[:, None] * inner_index[None, :]).astype(jnp.float32)
    )
    plan = (
        dft_tables(outer_len),
        dft_tables(inner_len),
        (jnp.cos(twiddle_angle), jnp.sin(twiddle_angle)),
    )
    cell_ids = jnp.arange(slice_cells, dtype=jnp.int32)
    projector = jnp.zeros((length, slice_cells), jnp.float32)
    for tap_number in range(ray_index.shape[1]):
        hit = (ray_index[0, tap_number][:, None] == cell_ids[None, :]).astype(jnp.float32)
        projector = projector + ray_weight[0, tap_number][:, None] * hit
    thickness = lax.dot_general(volume[0], projector, (((1,), (1,)), ((), ())), precision=highest)
    wavefront = jnp.stack([jnp.cos(thickness), jnp.sin(thickness)])
    row_spectrum = along_last(wavefront, plan, False)
    spectrum = along_last(exchange(row_spectrum, slabs, width), plan, False)
    position = jnp.arange(length, dtype=jnp.int32)
    row_freq = position // inner_len + outer_len * (position % inner_len)
    column_pos = lax.axis_index("slab") * width + jnp.arange(width, dtype=jnp.int32)
    column_freq = column_pos // inner_len + outer_len * (column_pos % inner_len)
    centered_rows = jnp.where(row_freq < length // 2, row_freq, row_freq - length)
    centered_cols = jnp.where(column_freq < length // 2, column_freq, column_freq - length)
    radius = (
        centered_cols[:, None] * centered_cols[:, None]
        + centered_rows[None, :] * centered_rows[None, :]
    ).astype(jnp.float32)
    phase = -math.pi * fresnel[:, None, None] * radius[None] / HOLOGRAM
    kernel_real = jnp.cos(phase)
    kernel_imag = jnp.sin(phase)
    propagated = jnp.stack(
        [
            kernel_real * spectrum[0] - kernel_imag * spectrum[1],
            kernel_real * spectrum[1] + kernel_imag * spectrum[0],
        ],
        axis=1,
    )
    column_fields = along_last(propagated, plan, True)
    fields = along_last(exchange(column_fields, slabs, width), plan, True)
    magnitude = jnp.sqrt(fields[:, 0] * fields[:, 0] + fields[:, 1] * fields[:, 1])
    factor = amplitude[0] / jnp.maximum(magnitude, mod_floor)
    moduli_rows = along_last(fields * factor[:, None], plan, False)
    moduli_spectra = along_last(exchange(moduli_rows, slabs, width), plan, False)
    total_real = jnp.sum(
        kernel_real * moduli_spectra[:, 0] + kernel_imag * moduli_spectra[:, 1], axis=0
    )
    total_imag = jnp.sum(
        kernel_real * moduli_spectra[:, 1] - kernel_imag * moduli_spectra[:, 0], axis=0
    )
    averaged = jnp.stack([total_real, total_imag]) / DISTANCES
    column_back = along_last(averaged, plan, True)
    back = along_last(exchange(column_back, slabs, width), plan, True)
    gradient = jnp.cos(thickness) * back[1] - jnp.sin(thickness) * back[0]
    bprojected = jnp.matmul(gradient, projector, precision=highest)
    volume_next = volume[0] + step_size * (
        bprojected - penalty * (volume[0] - consensus + scaled_dual[0])
    )
    combined = volume_next + scaled_dual[0]
    total = combined
    step = 1
    while step < groups:
        pairs = [(index, index ^ step) for index in range(groups)]
        total = total + lax.ppermute(total, "group", pairs)
        step *= 2
    consensus_next = total / groups
    dual_next = scaled_dual[0] + volume_next - consensus_next
    return (volume_next[None], consensus_next, dual_next[None])


def solution(mesh):
    placed = (
        P("group", "slab", None),
        P("slab", None),
        P("group", "slab", None),
        P("group", None, "slab", None),
        P(),
        P("group", None, None),
        P("group", None, None),
    )
    return jax.shard_map(
        shards,
        mesh=mesh,
        in_specs=placed,
        out_specs=(P("group", "slab", None), P("slab", None), P("group", "slab", None)),
        check_vma=False,
    )
```

```python
import math

import jax
import jax.numpy as jnp
from jax import lax
from jax.sharding import PartitionSpec as P

HOLOGRAM = 1024
DISTANCES = 4


step_size = 0.5
penalty = 0.5
mod_floor = 0.25
highest = lax.Precision.HIGHEST


def dft_tables(count):
    index = jnp.arange(count, dtype=jnp.int32)
    angle = 2.0 * math.pi / count * (index[:, None] * index[None, :] % count).astype(jnp.float32)
    return (jnp.cos(angle), jnp.sin(angle))


def complex_contract(real_part, imag_part, tables, form, inverse):
    cos_table, sin_table = tables
    real_cos = jnp.einsum(form, real_part, cos_table, precision=highest)
    real_sin = jnp.einsum(form, real_part, sin_table, precision=highest)
    imag_cos = jnp.einsum(form, imag_part, cos_table, precision=highest)
    imag_sin = jnp.einsum(form, imag_part, sin_table, precision=highest)
    if inverse:
        return (real_cos - imag_sin, imag_cos + real_sin)
    return (real_cos + imag_sin, imag_cos - real_sin)


def twiddle_apply(real_part, imag_part, twiddle, inverse):
    twiddle_cos, twiddle_sin = twiddle
    if inverse:
        return (
            real_part * twiddle_cos - imag_part * twiddle_sin,
            imag_part * twiddle_cos + real_part * twiddle_sin,
        )
    return (
        real_part * twiddle_cos + imag_part * twiddle_sin,
        imag_part * twiddle_cos - real_part * twiddle_sin,
    )


def along_last(values, plan, inverse):
    outer_tables, inner_tables, twiddle = plan
    outer_len = outer_tables[0].shape[0]
    inner_len = inner_tables[0].shape[0]
    real_part = values[..., 0, :, :]
    imag_part = values[..., 1, :, :]
    shape = real_part.shape
    length = shape[-1]
    real_part = real_part.reshape(shape[:-1] + (outer_len, inner_len))
    imag_part = imag_part.reshape(shape[:-1] + (outer_len, inner_len))
    outer_form = "...ab,ak->...kb"
    inner_form = "...ab,bl->...al"
    if inverse:
        real_part, imag_part = complex_contract(
            real_part, imag_part, inner_tables, inner_form, True
        )
        real_part, imag_part = twiddle_apply(real_part, imag_part, twiddle, True)
        real_part, imag_part = complex_contract(
            real_part, imag_part, outer_tables, outer_form, True
        )
    else:
        real_part, imag_part = complex_contract(
            real_part, imag_part, outer_tables, outer_form, False
        )
        real_part, imag_part = twiddle_apply(real_part, imag_part, twiddle, False)
        real_part, imag_part = complex_contract(
            real_part, imag_part, inner_tables, inner_form, False
        )
    result = jnp.stack([real_part.reshape(shape), imag_part.reshape(shape)], axis=-3)
    if inverse:
        return result * (1.0 / length)
    return result


def along_first(values, plan, inverse):
    outer_tables, inner_tables, twiddle = plan
    outer_len = outer_tables[0].shape[0]
    inner_len = inner_tables[0].shape[0]
    real_part = values[..., 0, :, :]
    imag_part = values[..., 1, :, :]
    shape = real_part.shape
    length = shape[-2]
    split_shape = shape[:-2] + (outer_len, inner_len, shape[-1])
    real_part = real_part.reshape(split_shape)
    imag_part = imag_part.reshape(split_shape)
    twiddle_cols = (twiddle[0][:, :, None], twiddle[1][:, :, None])
    outer_form = "...abw,ak->...kbw"
    inner_form = "...abw,bl->...alw"
    if inverse:
        real_part, imag_part = complex_contract(
            real_part, imag_part, inner_tables, inner_form, True
        )
        real_part, imag_part = twiddle_apply(real_part, imag_part, twiddle_cols, True)
        real_part, imag_part = complex_contract(
            real_part, imag_part, outer_tables, outer_form, True
        )
    else:
        real_part, imag_part = complex_contract(
            real_part, imag_part, outer_tables, outer_form, False
        )
        real_part, imag_part = twiddle_apply(real_part, imag_part, twiddle_cols, False)
        real_part, imag_part = complex_contract(
            real_part, imag_part, inner_tables, inner_form, False
        )
    result = jnp.stack([real_part.reshape(shape), imag_part.reshape(shape)], axis=-3)
    if inverse:
        return result * (1.0 / length)
    return result


def rows_to_columns(values, slabs, width):
    lead = values.shape[:-3]
    rank = len(lead)
    rows = values.shape[-2]
    blocks = values.reshape(lead + (2, rows, slabs, width))
    order = (rank, rank + 2, rank + 1) + tuple(range(rank)) + (rank + 3,)
    lanes = width
    for size in lead:
        lanes *= size
    outgoing = jnp.transpose(blocks, order).reshape(2, slabs, rows, lanes)
    incoming = lax.all_to_all(outgoing, "slab", split_axis=1, concat_axis=1, tiled=True)
    incoming = incoming.reshape(2, slabs * rows, lanes)
    return (incoming[0], incoming[1])


def columns_to_rows(real_part, imag_part, slabs, width, count):
    length = real_part.shape[0]
    rows = length // slabs
    outgoing = jnp.stack([real_part, imag_part]).reshape(2, slabs, rows, count * width)
    incoming = lax.all_to_all(outgoing, "slab", split_axis=1, concat_axis=1, tiled=True)
    incoming = incoming.reshape(2, slabs, rows, count, width)
    return jnp.transpose(incoming, (3, 0, 2, 1, 4)).reshape(count, 2, rows, slabs * width)


def along_columns(real_part, imag_part, plan, inverse):
    outer_tables, inner_tables, twiddle = plan
    outer_len = outer_tables[0].shape[0]
    inner_len = inner_tables[0].shape[0]
    length, lanes = real_part.shape

    def contract(tables, real_in, imag_in, axis):
        dims = (((0,), (axis,)), ((), ()))
        cos_table, sin_table = tables
        real_cos = lax.dot_general(cos_table, real_in, dims, precision=highest)
        real_sin = lax.dot_general(sin_table, real_in, dims, precision=highest)
        imag_cos = lax.dot_general(cos_table, imag_in, dims, precision=highest)
        imag_sin = lax.dot_general(sin_table, imag_in, dims, precision=highest)
        if inverse:
            return (real_cos - imag_sin, imag_cos + real_sin)
        return (real_cos + imag_sin, imag_cos - real_sin)

    if inverse:
        real_in = real_part.reshape(inner_len, outer_len, lanes)
        imag_in = imag_part.reshape(inner_len, outer_len, lanes)
        real_mid, imag_mid = contract(inner_tables, real_in, imag_in, 0)
        turn = (twiddle[0].T[:, :, None], twiddle[1].T[:, :, None])
        real_mid, imag_mid = twiddle_apply(real_mid, imag_mid, turn, True)
        real_out, imag_out = contract(outer_tables, real_mid, imag_mid, 1)
        scale = 1.0 / length
        return (real_out.reshape(length, lanes) * scale, imag_out.reshape(length, lanes) * scale)
    real_in = real_part.reshape(outer_len, inner_len, lanes)
    imag_in = imag_part.reshape(outer_len, inner_len, lanes)
    real_mid, imag_mid = contract(outer_tables, real_in, imag_in, 0)
    turn = (twiddle[0][:, :, None], twiddle[1][:, :, None])
    real_mid, imag_mid = twiddle_apply(real_mid, imag_mid, turn, False)
    real_out, imag_out = contract(inner_tables, real_mid, imag_mid, 1)
    return (real_out.reshape(length, lanes), imag_out.reshape(length, lanes))

def shards(volume, consensus, scaled_dual, amplitude, fresnel, ray_index, ray_weight):
    slice_cells = volume.shape[2]
    length = amplitude.shape[3]
    slabs = lax.axis_size("slab")
    width = length // slabs
    groups = lax.axis_size("group")
    inner_len = min(128, length)
    outer_len = length // inner_len
    outer_index = jnp.arange(outer_len, dtype=jnp.int32)
    inner_index = jnp.arange(inner_len, dtype=jnp.int32)
    twiddle_angle = (
        2.0 * math.pi / length * (outer_index[:, None] * inner_index[None, :]).astype(jnp.float32)
    )
    plan = (
        dft_tables(outer_len),
        dft_tables(inner_len),
        (jnp.cos(twiddle_angle), jnp.sin(twiddle_angle)),
    )
    cell_ids = jnp.arange(slice_cells, dtype=jnp.int32)
    projector = jnp.zeros((length, slice_cells), jnp.float32)
    for tap_number in range(ray_index.shape[1]):
        hit = (ray_index[0, tap_number][:, None] == cell_ids[None, :]).astype(jnp.float32)
        projector = projector + ray_weight[0, tap_number][:, None] * hit
    thickness = lax.dot_general(volume[0], projector, (((1,), (1,)), ((), ())), precision=highest)
    wavefront = jnp.stack([jnp.cos(thickness), jnp.sin(thickness)])
    row_spectrum = along_last(wavefront, plan, False)
    spectrum_real, spectrum_imag = along_columns(
        *rows_to_columns(row_spectrum, slabs, width), plan, False
    )
    kz = jnp.arange(length, dtype=jnp.int32)
    column_pos = lax.axis_index("slab") * width + jnp.arange(width, dtype=jnp.int32)
    column_freq = column_pos // inner_len + outer_len * (column_pos % inner_len)
    centered_rows = jnp.where(kz < length // 2, kz, kz - length)
    centered_cols = jnp.where(column_freq < length // 2, column_freq, column_freq - length)
    radius = (
        centered_rows[:, None] * centered_rows[:, None]
        + centered_cols[None, :] * centered_cols[None, :]
    ).astype(jnp.float32)
    phase = -math.pi * fresnel[None, :, None] * radius[:, None, :] / HOLOGRAM
    lanes = DISTANCES * width
    kernel_real = jnp.cos(phase).reshape(length, lanes)
    kernel_imag = jnp.sin(phase).reshape(length, lanes)
    spread_real = jnp.broadcast_to(
        spectrum_real[:, None, :], (length, DISTANCES, width)
    ).reshape(length, lanes)
    spread_imag = jnp.broadcast_to(
        spectrum_imag[:, None, :], (length, DISTANCES, width)
    ).reshape(length, lanes)
    field_real, field_imag = along_columns(
        kernel_real * spread_real - kernel_imag * spread_imag,
        kernel_real * spread_imag + kernel_imag * spread_real,
        plan,
        True,
    )
    fields = along_last(
        columns_to_rows(field_real, field_imag, slabs, width, DISTANCES), plan, True
    )
    magnitude = jnp.sqrt(fields[:, 0] * fields[:, 0] + fields[:, 1] * fields[:, 1])
    factor = amplitude[0] / jnp.maximum(magnitude, mod_floor)
    moduli_rows = along_last(fields * factor[:, None], plan, False)
    moduli_real, moduli_imag = along_columns(
        *rows_to_columns(moduli_rows, slabs, width), plan, False
    )
    total_real = jnp.sum(
        (kernel_real * moduli_real + kernel_imag * moduli_imag).reshape(
            length, DISTANCES, width
        ),
        axis=1,
    )
    total_imag = jnp.sum(
        (kernel_real * moduli_imag - kernel_imag * moduli_real).reshape(
            length, DISTANCES, width
        ),
        axis=1,
    )
    back_real, back_imag = along_columns(
        total_real / DISTANCES, total_imag / DISTANCES, plan, True
    )
    back = along_last(columns_to_rows(back_real, back_imag, slabs, width, 1)[0], plan, True)
    gradient = jnp.cos(thickness) * back[1] - jnp.sin(thickness) * back[0]
    bprojected = jnp.matmul(gradient, projector, precision=highest)
    volume_next = volume[0] + step_size * (
        bprojected - penalty * (volume[0] - consensus + scaled_dual[0])
    )
    combined = volume_next + scaled_dual[0]
    total = combined
    step = 1
    while step < groups:
        pairs = [(index, index ^ step) for index in range(groups)]
        total = total + lax.ppermute(total, "group", pairs)
        step *= 2
    consensus_next = total / groups
    dual_next = scaled_dual[0] + volume_next - consensus_next
    return (volume_next[None], consensus_next, dual_next[None])


def solution(mesh):
    placed = (
        P("group", "slab", None),
        P("slab", None),
        P("group", "slab", None),
        P("group", None, "slab", None),
        P(),
        P("group", None, None),
        P("group", None, None),
    )
    return jax.shard_map(
        shards,
        mesh=mesh,
        in_specs=placed,
        out_specs=(P("group", "slab", None), P("slab", None), P("group", "slab", None)),
        check_vma=False,
    )
```

```python
import math

import jax
import jax.numpy as jnp
from jax import lax
from jax.sharding import PartitionSpec as P

HOLOGRAM = 1024
DISTANCES = 4


step_size = 0.5
penalty = 0.5
mod_floor = 0.25
highest = lax.Precision.HIGHEST


def dft_tables(count):
    index = jnp.arange(count, dtype=jnp.int32)
    angle = 2.0 * math.pi / count * (index[:, None] * index[None, :] % count).astype(jnp.float32)
    return (jnp.cos(angle), jnp.sin(angle))


def complex_contract(real_part, imag_part, tables, form, inverse):
    cos_table, sin_table = tables
    real_cos = jnp.einsum(form, real_part, cos_table, precision=highest)
    real_sin = jnp.einsum(form, real_part, sin_table, precision=highest)
    imag_cos = jnp.einsum(form, imag_part, cos_table, precision=highest)
    imag_sin = jnp.einsum(form, imag_part, sin_table, precision=highest)
    if inverse:
        return (real_cos - imag_sin, imag_cos + real_sin)
    return (real_cos + imag_sin, imag_cos - real_sin)


def twiddle_apply(real_part, imag_part, twiddle, inverse):
    twiddle_cos, twiddle_sin = twiddle
    if inverse:
        return (
            real_part * twiddle_cos - imag_part * twiddle_sin,
            imag_part * twiddle_cos + real_part * twiddle_sin,
        )
    return (
        real_part * twiddle_cos + imag_part * twiddle_sin,
        imag_part * twiddle_cos - real_part * twiddle_sin,
    )


def along_last(values, plan, inverse):
    outer_tables, inner_tables, twiddle = plan
    outer_len = outer_tables[0].shape[0]
    inner_len = inner_tables[0].shape[0]
    real_part = values[..., 0, :, :]
    imag_part = values[..., 1, :, :]
    shape = real_part.shape
    length = shape[-1]
    real_part = real_part.reshape(shape[:-1] + (outer_len, inner_len))
    imag_part = imag_part.reshape(shape[:-1] + (outer_len, inner_len))
    outer_form = "...ab,ak->...kb"
    inner_form = "...ab,bl->...al"
    if inverse:
        real_part, imag_part = complex_contract(
            real_part, imag_part, inner_tables, inner_form, True
        )
        real_part, imag_part = twiddle_apply(real_part, imag_part, twiddle, True)
        real_part, imag_part = complex_contract(
            real_part, imag_part, outer_tables, outer_form, True
        )
    else:
        real_part, imag_part = complex_contract(
            real_part, imag_part, outer_tables, outer_form, False
        )
        real_part, imag_part = twiddle_apply(real_part, imag_part, twiddle, False)
        real_part, imag_part = complex_contract(
            real_part, imag_part, inner_tables, inner_form, False
        )
    result = jnp.stack([real_part.reshape(shape), imag_part.reshape(shape)], axis=-3)
    if inverse:
        return result * (1.0 / length)
    return result


def along_first(values, plan, inverse):
    outer_tables, inner_tables, twiddle = plan
    outer_len = outer_tables[0].shape[0]
    inner_len = inner_tables[0].shape[0]
    real_part = values[..., 0, :, :]
    imag_part = values[..., 1, :, :]
    shape = real_part.shape
    length = shape[-2]
    split_shape = shape[:-2] + (outer_len, inner_len, shape[-1])
    real_part = real_part.reshape(split_shape)
    imag_part = imag_part.reshape(split_shape)
    twiddle_cols = (twiddle[0][:, :, None], twiddle[1][:, :, None])
    outer_form = "...abw,ak->...kbw"
    inner_form = "...abw,bl->...alw"
    if inverse:
        real_part, imag_part = complex_contract(
            real_part, imag_part, inner_tables, inner_form, True
        )
        real_part, imag_part = twiddle_apply(real_part, imag_part, twiddle_cols, True)
        real_part, imag_part = complex_contract(
            real_part, imag_part, outer_tables, outer_form, True
        )
    else:
        real_part, imag_part = complex_contract(
            real_part, imag_part, outer_tables, outer_form, False
        )
        real_part, imag_part = twiddle_apply(real_part, imag_part, twiddle_cols, False)
        real_part, imag_part = complex_contract(
            real_part, imag_part, inner_tables, inner_form, False
        )
    result = jnp.stack([real_part.reshape(shape), imag_part.reshape(shape)], axis=-3)
    if inverse:
        return result * (1.0 / length)
    return result


def rows_to_columns(values, slabs, width):
    lead = values.shape[:-3]
    rank = len(lead)
    rows = values.shape[-2]
    parts = values.shape[-3]
    blocks = values.reshape(lead + (parts, rows, slabs, width))
    order = (rank, rank + 2, rank + 1) + tuple(range(rank)) + (rank + 3,)
    lanes = width
    for size in lead:
        lanes *= size
    outgoing = jnp.transpose(blocks, order).reshape(parts, slabs, rows, lanes)
    incoming = lax.all_to_all(outgoing, "slab", split_axis=1, concat_axis=1, tiled=True)
    incoming = incoming.reshape(parts, slabs * rows, lanes)
    return tuple(incoming[part] for part in range(parts))


def columns_to_rows(real_part, imag_part, slabs, width, count):
    length = real_part.shape[0]
    rows = length // slabs
    outgoing = jnp.stack([real_part, imag_part]).reshape(2, slabs, rows, count * width)
    incoming = lax.all_to_all(outgoing, "slab", split_axis=1, concat_axis=1, tiled=True)
    incoming = incoming.reshape(2, slabs, rows, count, width)
    return jnp.transpose(incoming, (3, 0, 2, 1, 4)).reshape(count, 2, rows, slabs * width)


def along_columns(real_part, imag_part, plan, inverse):
    outer_tables, inner_tables, twiddle = plan
    outer_len = outer_tables[0].shape[0]
    inner_len = inner_tables[0].shape[0]
    length, lanes = real_part.shape

    def contract(tables, real_in, imag_in, axis):
        dims = (((0,), (axis,)), ((), ()))
        cos_table, sin_table = tables
        real_cos = lax.dot_general(cos_table, real_in, dims, precision=highest)
        real_sin = lax.dot_general(sin_table, real_in, dims, precision=highest)
        imag_cos = lax.dot_general(cos_table, imag_in, dims, precision=highest)
        imag_sin = lax.dot_general(sin_table, imag_in, dims, precision=highest)
        if inverse:
            return (real_cos - imag_sin, imag_cos + real_sin)
        return (real_cos + imag_sin, imag_cos - real_sin)

    if inverse:
        real_in = real_part.reshape(inner_len, outer_len, lanes)
        imag_in = imag_part.reshape(inner_len, outer_len, lanes)
        real_mid, imag_mid = contract(inner_tables, real_in, imag_in, 0)
        turn = (twiddle[0].T[:, :, None], twiddle[1].T[:, :, None])
        real_mid, imag_mid = twiddle_apply(real_mid, imag_mid, turn, True)
        real_out, imag_out = contract(outer_tables, real_mid, imag_mid, 1)
        scale = 1.0 / length
        return (real_out.reshape(length, lanes) * scale, imag_out.reshape(length, lanes) * scale)
    real_in = real_part.reshape(outer_len, inner_len, lanes)
    imag_in = imag_part.reshape(outer_len, inner_len, lanes)
    real_mid, imag_mid = contract(outer_tables, real_in, imag_in, 0)
    turn = (twiddle[0][:, :, None], twiddle[1][:, :, None])
    real_mid, imag_mid = twiddle_apply(real_mid, imag_mid, turn, False)
    real_out, imag_out = contract(inner_tables, real_mid, imag_mid, 1)
    return (real_out.reshape(length, lanes), imag_out.reshape(length, lanes))

def shards(volume, consensus, scaled_dual, amplitude, fresnel, ray_index, ray_weight):
    slice_cells = volume.shape[2]
    length = amplitude.shape[3]
    slabs = lax.axis_size("slab")
    width = length // slabs
    groups = lax.axis_size("group")
    inner_len = min(128, length)
    outer_len = length // inner_len
    outer_index = jnp.arange(outer_len, dtype=jnp.int32)
    inner_index = jnp.arange(inner_len, dtype=jnp.int32)
    twiddle_angle = (
        2.0 * math.pi / length * (outer_index[:, None] * inner_index[None, :]).astype(jnp.float32)
    )
    plan = (
        dft_tables(outer_len),
        dft_tables(inner_len),
        (jnp.cos(twiddle_angle), jnp.sin(twiddle_angle)),
    )
    cell_ids = jnp.arange(slice_cells, dtype=jnp.int32)
    projector = jnp.zeros((length, slice_cells), jnp.float32)
    for tap_number in range(ray_index.shape[1]):
        hit = (ray_index[0, tap_number][:, None] == cell_ids[None, :]).astype(jnp.float32)
        projector = projector + ray_weight[0, tap_number][:, None] * hit
    thickness = lax.dot_general(volume[0], projector, (((1,), (1,)), ((), ())), precision=highest)
    wavefront = jnp.stack([jnp.cos(thickness), jnp.sin(thickness)])
    row_spectrum = along_last(wavefront, plan, False)
    position = jnp.arange(length, dtype=jnp.int32)
    row_freq = position // inner_len + outer_len * (position % inner_len)
    centered_u = jnp.where(row_freq < length // 2, row_freq, row_freq - length)
    phase_u = (
        -math.pi * fresnel[:, None] * (centered_u * centered_u).astype(jnp.float32)[None, :]
        / HOLOGRAM
    )
    row_kernel_real = jnp.cos(phase_u)[:, None, :]
    row_kernel_imag = jnp.sin(phase_u)[:, None, :]
    u_fields = along_last(
        jnp.stack(
            [
                row_kernel_real * row_spectrum[0] - row_kernel_imag * row_spectrum[1],
                row_kernel_real * row_spectrum[1] + row_kernel_imag * row_spectrum[0],
            ],
            axis=1,
        ),
        plan,
        True,
    )
    packed = jnp.concatenate([u_fields, amplitude[0][:, None]], axis=1)
    column_real, column_imag, column_amplitude = rows_to_columns(packed, slabs, width)
    centered_z = jnp.where(position < length // 2, position, position - length)
    phase_z = (
        -math.pi * fresnel[None, :, None]
        * (centered_z * centered_z).astype(jnp.float32)[:, None, None]
        / HOLOGRAM
    )
    lanes = DISTANCES * width
    phase_z = jnp.broadcast_to(phase_z, (length, DISTANCES, width)).reshape(length, lanes)
    kernel_real = jnp.cos(phase_z)
    kernel_imag = jnp.sin(phase_z)
    spectrum_real, spectrum_imag = along_columns(column_real, column_imag, plan, False)
    field_real, field_imag = along_columns(
        kernel_real * spectrum_real - kernel_imag * spectrum_imag,
        kernel_real * spectrum_imag + kernel_imag * spectrum_real,
        plan,
        True,
    )
    magnitude = jnp.sqrt(field_real * field_real + field_imag * field_imag)
    factor = column_amplitude / jnp.maximum(magnitude, mod_floor)
    moduli_real, moduli_imag = along_columns(field_real * factor, field_imag * factor, plan, False)
    turned_real, turned_imag = along_columns(
        kernel_real * moduli_real + kernel_imag * moduli_imag,
        kernel_real * moduli_imag - kernel_imag * moduli_real,
        plan,
        True,
    )
    row_moduli = along_last(
        columns_to_rows(turned_real, turned_imag, slabs, width, DISTANCES), plan, False
    )
    total_real = jnp.sum(
        row_kernel_real * row_moduli[:, 0] + row_kernel_imag * row_moduli[:, 1],
        axis=0,
    )
    total_imag = jnp.sum(
        row_kernel_real * row_moduli[:, 1] - row_kernel_imag * row_moduli[:, 0],
        axis=0,
    )
    back = along_last(jnp.stack([total_real, total_imag]) / DISTANCES, plan, True)
    gradient = jnp.cos(thickness) * back[1] - jnp.sin(thickness) * back[0]
    bprojected = jnp.matmul(gradient, projector, precision=highest)
    volume_next = volume[0] + step_size * (
        bprojected - penalty * (volume[0] - consensus + scaled_dual[0])
    )
    combined = volume_next + scaled_dual[0]
    total = combined
    step = 1
    while step < groups:
        pairs = [(index, index ^ step) for index in range(groups)]
        total = total + lax.ppermute(total, "group", pairs)
        step *= 2
    consensus_next = total / groups
    dual_next = scaled_dual[0] + volume_next - consensus_next
    return (volume_next[None], consensus_next, dual_next[None])


def solution(mesh):
    placed = (
        P("group", "slab", None),
        P("slab", None),
        P("group", "slab", None),
        P("group", None, "slab", None),
        P(),
        P("group", None, None),
        P("group", None, None),
    )
    return jax.shard_map(
        shards,
        mesh=mesh,
        in_specs=placed,
        out_specs=(P("group", "slab", None), P("slab", None), P("group", "slab", None)),
        check_vma=False,
    )
```

```python
import math

import jax
import jax.numpy as jnp
from jax import lax
from jax.sharding import PartitionSpec as P

HOLOGRAM = 1024
DISTANCES = 4


step_size = 0.5
penalty = 0.5
mod_floor = 0.25
highest = lax.Precision.HIGHEST


def dft_tables(count):
    index = jnp.arange(count, dtype=jnp.int32)
    angle = 2.0 * math.pi / count * (index[:, None] * index[None, :] % count).astype(jnp.float32)
    return (jnp.cos(angle), jnp.sin(angle))


def complex_contract(real_part, imag_part, tables, form, inverse):
    cos_table, sin_table = tables
    real_cos = jnp.einsum(form, real_part, cos_table, precision=highest)
    real_sin = jnp.einsum(form, real_part, sin_table, precision=highest)
    imag_cos = jnp.einsum(form, imag_part, cos_table, precision=highest)
    imag_sin = jnp.einsum(form, imag_part, sin_table, precision=highest)
    if inverse:
        return (real_cos - imag_sin, imag_cos + real_sin)
    return (real_cos + imag_sin, imag_cos - real_sin)


def twiddle_apply(real_part, imag_part, twiddle, inverse):
    twiddle_cos, twiddle_sin = twiddle
    if inverse:
        return (
            real_part * twiddle_cos - imag_part * twiddle_sin,
            imag_part * twiddle_cos + real_part * twiddle_sin,
        )
    return (
        real_part * twiddle_cos + imag_part * twiddle_sin,
        imag_part * twiddle_cos - real_part * twiddle_sin,
    )


def along_last(values, plan, inverse, split=False):
    outer_tables, inner_tables, twiddle = plan
    outer_len = outer_tables[0].shape[0]
    inner_len = inner_tables[0].shape[0]
    real_part = values[..., 0, :, :]
    imag_part = values[..., 1, :, :]
    shape = real_part.shape
    length = shape[-1]
    real_part = real_part.reshape(shape[:-1] + (outer_len, inner_len))
    imag_part = imag_part.reshape(shape[:-1] + (outer_len, inner_len))
    outer_form = "...ab,ak->...kb"
    inner_form = "...ab,bl->...al"
    if inverse:
        real_part, imag_part = complex_contract(
            real_part, imag_part, inner_tables, inner_form, True
        )
        real_part, imag_part = twiddle_apply(real_part, imag_part, twiddle, True)
        real_part, imag_part = complex_contract(
            real_part, imag_part, outer_tables, outer_form, True
        )
    else:
        real_part, imag_part = complex_contract(
            real_part, imag_part, outer_tables, outer_form, False
        )
        real_part, imag_part = twiddle_apply(real_part, imag_part, twiddle, False)
        real_part, imag_part = complex_contract(
            real_part, imag_part, inner_tables, inner_form, False
        )
    if split:
        result = jnp.stack([real_part, imag_part], axis=-4)
    else:
        result = jnp.stack([real_part.reshape(shape), imag_part.reshape(shape)], axis=-3)
    if inverse:
        return result * (1.0 / length)
    return result


def along_first(values, plan, inverse):
    outer_tables, inner_tables, twiddle = plan
    outer_len = outer_tables[0].shape[0]
    inner_len = inner_tables[0].shape[0]
    real_part = values[..., 0, :, :]
    imag_part = values[..., 1, :, :]
    shape = real_part.shape
    length = shape[-2]
    split_shape = shape[:-2] + (outer_len, inner_len, shape[-1])
    real_part = real_part.reshape(split_shape)
    imag_part = imag_part.reshape(split_shape)
    twiddle_cols = (twiddle[0][:, :, None], twiddle[1][:, :, None])
    outer_form = "...abw,ak->...kbw"
    inner_form = "...abw,bl->...alw"
    if inverse:
        real_part, imag_part = complex_contract(
            real_part, imag_part, inner_tables, inner_form, True
        )
        real_part, imag_part = twiddle_apply(real_part, imag_part, twiddle_cols, True)
        real_part, imag_part = complex_contract(
            real_part, imag_part, outer_tables, outer_form, True
        )
    else:
        real_part, imag_part = complex_contract(
            real_part, imag_part, outer_tables, outer_form, False
        )
        real_part, imag_part = twiddle_apply(real_part, imag_part, twiddle_cols, False)
        real_part, imag_part = complex_contract(
            real_part, imag_part, inner_tables, inner_form, False
        )
    result = jnp.stack([real_part.reshape(shape), imag_part.reshape(shape)], axis=-3)
    if inverse:
        return result * (1.0 / length)
    return result


def rows_to_columns(values, slabs, width):
    lead = values.shape[:-3]
    rank = len(lead)
    rows = values.shape[-2]
    parts = values.shape[-3]
    blocks = values.reshape(lead + (parts, rows, slabs, width))
    order = (rank, rank + 2, rank + 1) + tuple(range(rank)) + (rank + 3,)
    lanes = width
    for size in lead:
        lanes *= size
    outgoing = jnp.transpose(blocks, order).reshape(parts, slabs, rows, lanes)
    incoming = lax.all_to_all(outgoing, "slab", split_axis=1, concat_axis=1, tiled=True)
    incoming = incoming.reshape(parts, slabs * rows, lanes)
    return tuple(incoming[part] for part in range(parts))


def columns_to_rows(real_part, imag_part, slabs, width, count):
    length = real_part.shape[0]
    rows = length // slabs
    outgoing = jnp.stack([real_part, imag_part]).reshape(2, slabs, rows, count * width)
    incoming = lax.all_to_all(outgoing, "slab", split_axis=1, concat_axis=1, tiled=True)
    incoming = incoming.reshape(2, slabs, rows, count, width)
    return jnp.transpose(incoming, (3, 0, 2, 1, 4)).reshape(count, 2, rows, slabs * width)


def along_columns(real_part, imag_part, plan, inverse):
    outer_tables, inner_tables, twiddle = plan
    outer_len = outer_tables[0].shape[0]
    inner_len = inner_tables[0].shape[0]
    length, lanes = real_part.shape

    def contract(tables, real_in, imag_in, axis):
        dims = (((0,), (axis,)), ((), ()))
        cos_table, sin_table = tables
        real_cos = lax.dot_general(cos_table, real_in, dims, precision=highest)
        real_sin = lax.dot_general(sin_table, real_in, dims, precision=highest)
        imag_cos = lax.dot_general(cos_table, imag_in, dims, precision=highest)
        imag_sin = lax.dot_general(sin_table, imag_in, dims, precision=highest)
        if inverse:
            return (real_cos - imag_sin, imag_cos + real_sin)
        return (real_cos + imag_sin, imag_cos - real_sin)

    if inverse:
        real_in = real_part.reshape(inner_len, outer_len, lanes)
        imag_in = imag_part.reshape(inner_len, outer_len, lanes)
        real_mid, imag_mid = contract(inner_tables, real_in, imag_in, 0)
        turn = (twiddle[0].T[:, :, None], twiddle[1].T[:, :, None])
        real_mid, imag_mid = twiddle_apply(real_mid, imag_mid, turn, True)
        real_out, imag_out = contract(outer_tables, real_mid, imag_mid, 1)
        scale = 1.0 / length
        return (real_out.reshape(length, lanes) * scale, imag_out.reshape(length, lanes) * scale)
    real_in = real_part.reshape(outer_len, inner_len, lanes)
    imag_in = imag_part.reshape(outer_len, inner_len, lanes)
    real_mid, imag_mid = contract(outer_tables, real_in, imag_in, 0)
    turn = (twiddle[0][:, :, None], twiddle[1][:, :, None])
    real_mid, imag_mid = twiddle_apply(real_mid, imag_mid, turn, False)
    real_out, imag_out = contract(inner_tables, real_mid, imag_mid, 1)
    return (real_out.reshape(length, lanes), imag_out.reshape(length, lanes))

def regroup_to_columns(values, width):
    depth, parts, rows, chunks, inner = values.shape
    per = inner // width
    lanes = depth * width
    inner_index = jnp.arange(inner, dtype=jnp.int32)
    out_index = jnp.arange(per * lanes, dtype=jnp.int32)
    out_group = out_index // lanes
    out_depth = (out_index // width) % depth
    out_cell = out_group * width + out_index % width
    depth_index = jnp.arange(depth, dtype=jnp.int32)
    permutation = (
        (depth_index[:, None, None] == out_depth[None, None, :])
        & (inner_index[None, :, None] == out_cell[None, None, :])
    ).astype(jnp.float32)
    moved = lax.dot_general(
        values, permutation, (((0, 4), (0, 1)), ((), ())), precision=highest
    )
    moved = moved.reshape(parts, rows, chunks, per, lanes)
    return jnp.transpose(moved, (2, 3, 0, 1, 4)).reshape(chunks * per, parts, rows, lanes)


def shards(volume, consensus, scaled_dual, amplitude, fresnel, ray_index, ray_weight):
    slice_cells = volume.shape[2]
    length = amplitude.shape[3]
    slabs = lax.axis_size("slab")
    width = length // slabs
    groups = lax.axis_size("group")
    inner_len = min(128, length)
    outer_len = length // inner_len
    outer_index = jnp.arange(outer_len, dtype=jnp.int32)
    inner_index = jnp.arange(inner_len, dtype=jnp.int32)
    twiddle_angle = (
        2.0 * math.pi / length * (outer_index[:, None] * inner_index[None, :]).astype(jnp.float32)
    )
    plan = (
        dft_tables(outer_len),
        dft_tables(inner_len),
        (jnp.cos(twiddle_angle), jnp.sin(twiddle_angle)),
    )
    cell_ids = jnp.arange(slice_cells, dtype=jnp.int32)
    projector = jnp.zeros((length, slice_cells), jnp.float32)
    for tap_number in range(ray_index.shape[1]):
        hit = (ray_index[0, tap_number][:, None] == cell_ids[None, :]).astype(jnp.float32)
        projector = projector + ray_weight[0, tap_number][:, None] * hit
    thickness = lax.dot_general(volume[0], projector, (((1,), (1,)), ((), ())), precision=highest)
    wavefront = jnp.stack([jnp.cos(thickness), jnp.sin(thickness)])
    row_spectrum = along_last(wavefront, plan, False)
    position = jnp.arange(length, dtype=jnp.int32)
    row_freq = position // inner_len + outer_len * (position % inner_len)
    centered_u = jnp.where(row_freq < length // 2, row_freq, row_freq - length)
    phase_u = (
        -math.pi * fresnel[:, None] * (centered_u * centered_u).astype(jnp.float32)[None, :]
        / HOLOGRAM
    )
    row_kernel_real = jnp.cos(phase_u)[:, None, :]
    row_kernel_imag = jnp.sin(phase_u)[:, None, :]
    u_fields = along_last(
        jnp.stack(
            [
                row_kernel_real * row_spectrum[0] - row_kernel_imag * row_spectrum[1],
                row_kernel_real * row_spectrum[1] + row_kernel_imag * row_spectrum[0],
            ],
            axis=1,
        ),
        plan,
        True,
        split=True,
    )
    measured = amplitude[0].reshape((DISTANCES, 1, amplitude.shape[2]) + u_fields.shape[-2:])
    packed = jnp.concatenate(
        [regroup_to_columns(u_fields, width), regroup_to_columns(measured, width)], axis=1
    )
    incoming = lax.all_to_all(packed, "slab", split_axis=0, concat_axis=0, tiled=True)
    column_real, column_imag, column_amplitude = (
        incoming[:, part].reshape(length, DISTANCES * width) for part in range(3)
    )
    centered_z = jnp.where(position < length // 2, position, position - length)
    phase_z = (
        -math.pi * fresnel[None, :, None]
        * (centered_z * centered_z).astype(jnp.float32)[:, None, None]
        / HOLOGRAM
    )
    lanes = DISTANCES * width
    phase_z = jnp.broadcast_to(phase_z, (length, DISTANCES, width)).reshape(length, lanes)
    kernel_real = jnp.cos(phase_z)
    kernel_imag = jnp.sin(phase_z)
    spectrum_real, spectrum_imag = along_columns(column_real, column_imag, plan, False)
    field_real, field_imag = along_columns(
        kernel_real * spectrum_real - kernel_imag * spectrum_imag,
        kernel_real * spectrum_imag + kernel_imag * spectrum_real,
        plan,
        True,
    )
    magnitude = jnp.sqrt(field_real * field_real + field_imag * field_imag)
    factor = column_amplitude / jnp.maximum(magnitude, mod_floor)
    moduli_real, moduli_imag = along_columns(field_real * factor, field_imag * factor, plan, False)
    turned_real, turned_imag = along_columns(
        kernel_real * moduli_real + kernel_imag * moduli_imag,
        kernel_real * moduli_imag - kernel_imag * moduli_real,
        plan,
        True,
    )
    row_moduli = along_last(
        columns_to_rows(turned_real, turned_imag, slabs, width, DISTANCES), plan, False
    )
    total_real = jnp.sum(
        row_kernel_real * row_moduli[:, 0] + row_kernel_imag * row_moduli[:, 1],
        axis=0,
    )
    total_imag = jnp.sum(
        row_kernel_real * row_moduli[:, 1] - row_kernel_imag * row_moduli[:, 0],
        axis=0,
    )
    back = along_last(jnp.stack([total_real, total_imag]) / DISTANCES, plan, True)
    gradient = jnp.cos(thickness) * back[1] - jnp.sin(thickness) * back[0]
    bprojected = jnp.matmul(gradient, projector, precision=highest)
    volume_next = volume[0] + step_size * (
        bprojected - penalty * (volume[0] - consensus + scaled_dual[0])
    )
    combined = volume_next + scaled_dual[0]
    total = combined
    step = 1
    while step < groups:
        pairs = [(index, index ^ step) for index in range(groups)]
        total = total + lax.ppermute(total, "group", pairs)
        step *= 2
    consensus_next = total / groups
    dual_next = scaled_dual[0] + volume_next - consensus_next
    return (volume_next[None], consensus_next, dual_next[None])


def solution(mesh):
    placed = (
        P("group", "slab", None),
        P("slab", None),
        P("group", "slab", None),
        P("group", None, "slab", None),
        P(),
        P("group", None, None),
        P("group", None, None),
    )
    return jax.shard_map(
        shards,
        mesh=mesh,
        in_specs=placed,
        out_specs=(P("group", "slab", None), P("slab", None), P("group", "slab", None)),
        check_vma=False,
    )
```

```python
import math

import jax
import jax.numpy as jnp
from jax import lax
from jax.sharding import PartitionSpec as P

HOLOGRAM = 1024
DISTANCES = 4


step_size = 0.5
penalty = 0.5
mod_floor = 0.25
highest = lax.Precision.HIGHEST


def dft_tables(count):
    index = jnp.arange(count, dtype=jnp.int32)
    angle = 2.0 * math.pi / count * (index[:, None] * index[None, :] % count).astype(jnp.float32)
    return (jnp.cos(angle), jnp.sin(angle))


def complex_contract(real_part, imag_part, tables, form, inverse):
    cos_table, sin_table = tables
    real_cos = jnp.einsum(form, real_part, cos_table, precision=highest)
    real_sin = jnp.einsum(form, real_part, sin_table, precision=highest)
    imag_cos = jnp.einsum(form, imag_part, cos_table, precision=highest)
    imag_sin = jnp.einsum(form, imag_part, sin_table, precision=highest)
    if inverse:
        return (real_cos - imag_sin, imag_cos + real_sin)
    return (real_cos + imag_sin, imag_cos - real_sin)


def twiddle_apply(real_part, imag_part, twiddle, inverse):
    twiddle_cos, twiddle_sin = twiddle
    if inverse:
        return (
            real_part * twiddle_cos - imag_part * twiddle_sin,
            imag_part * twiddle_cos + real_part * twiddle_sin,
        )
    return (
        real_part * twiddle_cos + imag_part * twiddle_sin,
        imag_part * twiddle_cos - real_part * twiddle_sin,
    )


def along_last(values, plan, inverse, split=False, split_in=False):
    outer_tables, inner_tables, twiddle = plan
    outer_len = outer_tables[0].shape[0]
    inner_len = inner_tables[0].shape[0]
    if split_in:
        real_part = values[..., 0, :, :, :]
        imag_part = values[..., 1, :, :, :]
        shape = real_part.shape[:-2] + (outer_len * inner_len,)
    else:
        real_part = values[..., 0, :, :]
        imag_part = values[..., 1, :, :]
        shape = real_part.shape
    length = shape[-1]
    real_part = real_part.reshape(shape[:-1] + (outer_len, inner_len))
    imag_part = imag_part.reshape(shape[:-1] + (outer_len, inner_len))
    outer_form = "...ab,ak->...kb"
    inner_form = "...ab,bl->...al"
    if inverse:
        real_part, imag_part = complex_contract(
            real_part, imag_part, inner_tables, inner_form, True
        )
        real_part, imag_part = twiddle_apply(real_part, imag_part, twiddle, True)
        real_part, imag_part = complex_contract(
            real_part, imag_part, outer_tables, outer_form, True
        )
    else:
        real_part, imag_part = complex_contract(
            real_part, imag_part, outer_tables, outer_form, False
        )
        real_part, imag_part = twiddle_apply(real_part, imag_part, twiddle, False)
        real_part, imag_part = complex_contract(
            real_part, imag_part, inner_tables, inner_form, False
        )
    if split:
        result = jnp.stack([real_part, imag_part], axis=-4)
    else:
        result = jnp.stack([real_part.reshape(shape), imag_part.reshape(shape)], axis=-3)
    if inverse:
        return result * (1.0 / length)
    return result


def along_first(values, plan, inverse):
    outer_tables, inner_tables, twiddle = plan
    outer_len = outer_tables[0].shape[0]
    inner_len = inner_tables[0].shape[0]
    real_part = values[..., 0, :, :]
    imag_part = values[..., 1, :, :]
    shape = real_part.shape
    length = shape[-2]
    split_shape = shape[:-2] + (outer_len, inner_len, shape[-1])
    real_part = real_part.reshape(split_shape)
    imag_part = imag_part.reshape(split_shape)
    twiddle_cols = (twiddle[0][:, :, None], twiddle[1][:, :, None])
    outer_form = "...abw,ak->...kbw"
    inner_form = "...abw,bl->...alw"
    if inverse:
        real_part, imag_part = complex_contract(
            real_part, imag_part, inner_tables, inner_form, True
        )
        real_part, imag_part = twiddle_apply(real_part, imag_part, twiddle_cols, True)
        real_part, imag_part = complex_contract(
            real_part, imag_part, outer_tables, outer_form, True
        )
    else:
        real_part, imag_part = complex_contract(
            real_part, imag_part, outer_tables, outer_form, False
        )
        real_part, imag_part = twiddle_apply(real_part, imag_part, twiddle_cols, False)
        real_part, imag_part = complex_contract(
            real_part, imag_part, inner_tables, inner_form, False
        )
    result = jnp.stack([real_part.reshape(shape), imag_part.reshape(shape)], axis=-3)
    if inverse:
        return result * (1.0 / length)
    return result


def rows_to_columns(values, slabs, width):
    lead = values.shape[:-3]
    rank = len(lead)
    rows = values.shape[-2]
    parts = values.shape[-3]
    blocks = values.reshape(lead + (parts, rows, slabs, width))
    order = (rank, rank + 2, rank + 1) + tuple(range(rank)) + (rank + 3,)
    lanes = width
    for size in lead:
        lanes *= size
    outgoing = jnp.transpose(blocks, order).reshape(parts, slabs, rows, lanes)
    incoming = lax.all_to_all(outgoing, "slab", split_axis=1, concat_axis=1, tiled=True)
    incoming = incoming.reshape(parts, slabs * rows, lanes)
    return tuple(incoming[part] for part in range(parts))


def columns_to_rows(real_part, imag_part, slabs, width, count):
    length = real_part.shape[0]
    rows = length // slabs
    outgoing = jnp.stack([real_part, imag_part]).reshape(2, slabs, rows, count * width)
    incoming = lax.all_to_all(outgoing, "slab", split_axis=1, concat_axis=1, tiled=True)
    incoming = incoming.reshape(2, slabs, rows, count, width)
    return jnp.transpose(incoming, (3, 0, 2, 1, 4)).reshape(count, 2, rows, slabs * width)


def along_columns(real_part, imag_part, plan, inverse):
    outer_tables, inner_tables, twiddle = plan
    outer_len = outer_tables[0].shape[0]
    inner_len = inner_tables[0].shape[0]
    length, lanes = real_part.shape

    def contract(tables, real_in, imag_in, axis):
        dims = (((0,), (axis,)), ((), ()))
        cos_table, sin_table = tables
        real_cos = lax.dot_general(cos_table, real_in, dims, precision=highest)
        real_sin = lax.dot_general(sin_table, real_in, dims, precision=highest)
        imag_cos = lax.dot_general(cos_table, imag_in, dims, precision=highest)
        imag_sin = lax.dot_general(sin_table, imag_in, dims, precision=highest)
        if inverse:
            return (real_cos - imag_sin, imag_cos + real_sin)
        return (real_cos + imag_sin, imag_cos - real_sin)

    if inverse:
        real_in = real_part.reshape(inner_len, outer_len, lanes)
        imag_in = imag_part.reshape(inner_len, outer_len, lanes)
        real_mid, imag_mid = contract(inner_tables, real_in, imag_in, 0)
        turn = (twiddle[0].T[:, :, None], twiddle[1].T[:, :, None])
        real_mid, imag_mid = twiddle_apply(real_mid, imag_mid, turn, True)
        real_out, imag_out = contract(outer_tables, real_mid, imag_mid, 1)
        scale = 1.0 / length
        return (real_out.reshape(length, lanes) * scale, imag_out.reshape(length, lanes) * scale)
    real_in = real_part.reshape(outer_len, inner_len, lanes)
    imag_in = imag_part.reshape(outer_len, inner_len, lanes)
    real_mid, imag_mid = contract(outer_tables, real_in, imag_in, 0)
    turn = (twiddle[0][:, :, None], twiddle[1][:, :, None])
    real_mid, imag_mid = twiddle_apply(real_mid, imag_mid, turn, False)
    real_out, imag_out = contract(inner_tables, real_mid, imag_mid, 1)
    return (real_out.reshape(length, lanes), imag_out.reshape(length, lanes))

def regroup_to_columns(values, width):
    depth, parts, rows, chunks, inner = values.shape
    per = inner // width
    lanes = depth * width
    inner_index = jnp.arange(inner, dtype=jnp.int32)
    out_index = jnp.arange(per * lanes, dtype=jnp.int32)
    out_group = out_index // lanes
    out_depth = (out_index // width) % depth
    out_cell = out_group * width + out_index % width
    depth_index = jnp.arange(depth, dtype=jnp.int32)
    permutation = (
        (depth_index[:, None, None] == out_depth[None, None, :])
        & (inner_index[None, :, None] == out_cell[None, None, :])
    ).astype(jnp.float32)
    moved = lax.dot_general(
        values, permutation, (((0, 4), (0, 1)), ((), ())), precision=highest
    )
    moved = moved.reshape(parts, rows, chunks, per, lanes)
    return jnp.transpose(moved, (2, 3, 0, 1, 4)).reshape(chunks * per, parts, rows, lanes)


def regroup_to_rows(real_part, imag_part, slabs, width, count):
    length, lanes = real_part.shape
    rows = length // slabs
    inner = 128
    per = inner // width
    chunks = slabs // per
    outgoing = jnp.transpose(
        jnp.stack([real_part, imag_part]).reshape(2, slabs, rows, lanes), (1, 0, 2, 3)
    )
    incoming = lax.all_to_all(outgoing, "slab", split_axis=0, concat_axis=0, tiled=True)
    incoming = incoming.reshape(chunks, per, 2, rows, lanes)
    lane_index = jnp.arange(lanes, dtype=jnp.int32)
    out_index = jnp.arange(count * inner, dtype=jnp.int32)
    out_depth = out_index // inner
    out_group = (out_index % inner) // width
    out_cell = out_index % width
    group_index = jnp.arange(per, dtype=jnp.int32)
    permutation = (
        (group_index[:, None, None] == out_group[None, None, :])
        & ((lane_index // width)[None, :, None] == out_depth[None, None, :])
        & ((lane_index % width)[None, :, None] == out_cell[None, None, :])
    ).astype(jnp.float32)
    moved = lax.dot_general(
        incoming, permutation, (((1, 4), (0, 1)), ((), ())), precision=highest
    )
    moved = moved.reshape(chunks, 2, rows, count, inner)
    return jnp.transpose(moved, (3, 1, 2, 0, 4))


def shards(volume, consensus, scaled_dual, amplitude, fresnel, ray_index, ray_weight):
    slice_cells = volume.shape[2]
    length = amplitude.shape[3]
    slabs = lax.axis_size("slab")
    width = length // slabs
    groups = lax.axis_size("group")
    inner_len = min(128, length)
    outer_len = length // inner_len
    outer_index = jnp.arange(outer_len, dtype=jnp.int32)
    inner_index = jnp.arange(inner_len, dtype=jnp.int32)
    twiddle_angle = (
        2.0 * math.pi / length * (outer_index[:, None] * inner_index[None, :]).astype(jnp.float32)
    )
    plan = (
        dft_tables(outer_len),
        dft_tables(inner_len),
        (jnp.cos(twiddle_angle), jnp.sin(twiddle_angle)),
    )
    cell_ids = jnp.arange(slice_cells, dtype=jnp.int32)
    projector = jnp.zeros((length, slice_cells), jnp.float32)
    for tap_number in range(ray_index.shape[1]):
        hit = (ray_index[0, tap_number][:, None] == cell_ids[None, :]).astype(jnp.float32)
        projector = projector + ray_weight[0, tap_number][:, None] * hit
    thickness = lax.dot_general(volume[0], projector, (((1,), (1,)), ((), ())), precision=highest)
    wavefront = jnp.stack([jnp.cos(thickness), jnp.sin(thickness)])
    row_spectrum = along_last(wavefront, plan, False)
    position = jnp.arange(length, dtype=jnp.int32)
    row_freq = position // inner_len + outer_len * (position % inner_len)
    centered_u = jnp.where(row_freq < length // 2, row_freq, row_freq - length)
    phase_u = (
        -math.pi * fresnel[:, None] * (centered_u * centered_u).astype(jnp.float32)[None, :]
        / HOLOGRAM
    )
    row_kernel_real = jnp.cos(phase_u)[:, None, :]
    row_kernel_imag = jnp.sin(phase_u)[:, None, :]
    u_fields = along_last(
        jnp.stack(
            [
                row_kernel_real * row_spectrum[0] - row_kernel_imag * row_spectrum[1],
                row_kernel_real * row_spectrum[1] + row_kernel_imag * row_spectrum[0],
            ],
            axis=1,
        ),
        plan,
        True,
        split=True,
    )
    measured = amplitude[0].reshape((DISTANCES, 1, amplitude.shape[2]) + u_fields.shape[-2:])
    packed = jnp.concatenate(
        [regroup_to_columns(u_fields, width), regroup_to_columns(measured, width)], axis=1
    )
    incoming = lax.all_to_all(packed, "slab", split_axis=0, concat_axis=0, tiled=True)
    column_real, column_imag, column_amplitude = (
        incoming[:, part].reshape(length, DISTANCES * width) for part in range(3)
    )
    centered_z = jnp.where(position < length // 2, position, position - length)
    phase_z = (
        -math.pi * fresnel[None, :, None]
        * (centered_z * centered_z).astype(jnp.float32)[:, None, None]
        / HOLOGRAM
    )
    lanes = DISTANCES * width
    phase_z = jnp.broadcast_to(phase_z, (length, DISTANCES, width)).reshape(length, lanes)
    kernel_real = jnp.cos(phase_z)
    kernel_imag = jnp.sin(phase_z)
    spectrum_real, spectrum_imag = along_columns(column_real, column_imag, plan, False)
    field_real, field_imag = along_columns(
        kernel_real * spectrum_real - kernel_imag * spectrum_imag,
        kernel_real * spectrum_imag + kernel_imag * spectrum_real,
        plan,
        True,
    )
    magnitude = jnp.sqrt(field_real * field_real + field_imag * field_imag)
    factor = column_amplitude / jnp.maximum(magnitude, mod_floor)
    moduli_real, moduli_imag = along_columns(field_real * factor, field_imag * factor, plan, False)
    turned_real, turned_imag = along_columns(
        kernel_real * moduli_real + kernel_imag * moduli_imag,
        kernel_real * moduli_imag - kernel_imag * moduli_real,
        plan,
        True,
    )
    row_moduli = along_last(
        regroup_to_rows(turned_real, turned_imag, slabs, width, DISTANCES),
        plan,
        False,
        split_in=True,
    )
    total_real = jnp.sum(
        row_kernel_real * row_moduli[:, 0] + row_kernel_imag * row_moduli[:, 1],
        axis=0,
    )
    total_imag = jnp.sum(
        row_kernel_real * row_moduli[:, 1] - row_kernel_imag * row_moduli[:, 0],
        axis=0,
    )
    back = along_last(jnp.stack([total_real, total_imag]) / DISTANCES, plan, True)
    gradient = jnp.cos(thickness) * back[1] - jnp.sin(thickness) * back[0]
    bprojected = jnp.matmul(gradient, projector, precision=highest)
    volume_next = volume[0] + step_size * (
        bprojected - penalty * (volume[0] - consensus + scaled_dual[0])
    )
    combined = volume_next + scaled_dual[0]
    total = combined
    step = 1
    while step < groups:
        pairs = [(index, index ^ step) for index in range(groups)]
        total = total + lax.ppermute(total, "group", pairs)
        step *= 2
    consensus_next = total / groups
    dual_next = scaled_dual[0] + volume_next - consensus_next
    return (volume_next[None], consensus_next, dual_next[None])


def solution(mesh):
    placed = (
        P("group", "slab", None),
        P("slab", None),
        P("group", "slab", None),
        P("group", None, "slab", None),
        P(),
        P("group", None, None),
        P("group", None, None),
    )
    return jax.shard_map(
        shards,
        mesh=mesh,
        in_specs=placed,
        out_specs=(P("group", "slab", None), P("slab", None), P("group", "slab", None)),
        check_vma=False,
    )
```

```python
import math

import jax
import jax.numpy as jnp
from jax import lax
from jax.sharding import PartitionSpec as P

HOLOGRAM = 1024
DISTANCES = 4


step_size = 0.5
penalty = 0.5
mod_floor = 0.25
highest = lax.Precision.HIGHEST


def dft_tables(count):
    index = jnp.arange(count, dtype=jnp.int32)
    angle = 2.0 * math.pi / count * (index[:, None] * index[None, :] % count).astype(jnp.float32)
    return (jnp.cos(angle), jnp.sin(angle))


def complex_contract(real_part, imag_part, tables, form, inverse):
    joined = jnp.concatenate(tables, axis=1)
    count = tables[0].shape[1]
    out_spec = form.split("->")[1]
    axis = out_spec.index(form.split(",")[1][1]) - len(out_spec)
    real_both = jnp.einsum(form, real_part, joined, precision=highest)
    imag_both = jnp.einsum(form, imag_part, joined, precision=highest)
    real_cos = lax.slice_in_dim(real_both, 0, count, axis=axis)
    real_sin = lax.slice_in_dim(real_both, count, 2 * count, axis=axis)
    imag_cos = lax.slice_in_dim(imag_both, 0, count, axis=axis)
    imag_sin = lax.slice_in_dim(imag_both, count, 2 * count, axis=axis)
    if inverse:
        return (real_cos - imag_sin, imag_cos + real_sin)
    return (real_cos + imag_sin, imag_cos - real_sin)


def twiddle_apply(real_part, imag_part, twiddle, inverse):
    twiddle_cos, twiddle_sin = twiddle
    if inverse:
        return (
            real_part * twiddle_cos - imag_part * twiddle_sin,
            imag_part * twiddle_cos + real_part * twiddle_sin,
        )
    return (
        real_part * twiddle_cos + imag_part * twiddle_sin,
        imag_part * twiddle_cos - real_part * twiddle_sin,
    )


def along_last(values, plan, inverse, split=False, split_in=False):
    outer_tables, inner_tables, twiddle = plan
    outer_len = outer_tables[0].shape[0]
    inner_len = inner_tables[0].shape[0]
    if split_in:
        real_part = values[..., 0, :, :, :]
        imag_part = values[..., 1, :, :, :]
        shape = real_part.shape[:-2] + (outer_len * inner_len,)
    else:
        real_part = values[..., 0, :, :]
        imag_part = values[..., 1, :, :]
        shape = real_part.shape
    length = shape[-1]
    real_part = real_part.reshape(shape[:-1] + (outer_len, inner_len))
    imag_part = imag_part.reshape(shape[:-1] + (outer_len, inner_len))
    outer_form = "...ab,ak->...kb"
    inner_form = "...ab,bl->...al"
    if inverse:
        real_part, imag_part = complex_contract(
            real_part, imag_part, inner_tables, inner_form, True
        )
        real_part, imag_part = twiddle_apply(real_part, imag_part, twiddle, True)
        real_part, imag_part = complex_contract(
            real_part, imag_part, outer_tables, outer_form, True
        )
    else:
        real_part, imag_part = complex_contract(
            real_part, imag_part, outer_tables, outer_form, False
        )
        real_part, imag_part = twiddle_apply(real_part, imag_part, twiddle, False)
        real_part, imag_part = complex_contract(
            real_part, imag_part, inner_tables, inner_form, False
        )
    if split:
        result = jnp.stack([real_part, imag_part], axis=-4)
    else:
        result = jnp.stack([real_part.reshape(shape), imag_part.reshape(shape)], axis=-3)
    if inverse:
        return result * (1.0 / length)
    return result


def along_first(values, plan, inverse):
    outer_tables, inner_tables, twiddle = plan
    outer_len = outer_tables[0].shape[0]
    inner_len = inner_tables[0].shape[0]
    real_part = values[..., 0, :, :]
    imag_part = values[..., 1, :, :]
    shape = real_part.shape
    length = shape[-2]
    split_shape = shape[:-2] + (outer_len, inner_len, shape[-1])
    real_part = real_part.reshape(split_shape)
    imag_part = imag_part.reshape(split_shape)
    twiddle_cols = (twiddle[0][:, :, None], twiddle[1][:, :, None])
    outer_form = "...abw,ak->...kbw"
    inner_form = "...abw,bl->...alw"
    if inverse:
        real_part, imag_part = complex_contract(
            real_part, imag_part, inner_tables, inner_form, True
        )
        real_part, imag_part = twiddle_apply(real_part, imag_part, twiddle_cols, True)
        real_part, imag_part = complex_contract(
            real_part, imag_part, outer_tables, outer_form, True
        )
    else:
        real_part, imag_part = complex_contract(
            real_part, imag_part, outer_tables, outer_form, False
        )
        real_part, imag_part = twiddle_apply(real_part, imag_part, twiddle_cols, False)
        real_part, imag_part = complex_contract(
            real_part, imag_part, inner_tables, inner_form, False
        )
    result = jnp.stack([real_part.reshape(shape), imag_part.reshape(shape)], axis=-3)
    if inverse:
        return result * (1.0 / length)
    return result


def rows_to_columns(values, slabs, width):
    lead = values.shape[:-3]
    rank = len(lead)
    rows = values.shape[-2]
    parts = values.shape[-3]
    blocks = values.reshape(lead + (parts, rows, slabs, width))
    order = (rank, rank + 2, rank + 1) + tuple(range(rank)) + (rank + 3,)
    lanes = width
    for size in lead:
        lanes *= size
    outgoing = jnp.transpose(blocks, order).reshape(parts, slabs, rows, lanes)
    incoming = lax.all_to_all(outgoing, "slab", split_axis=1, concat_axis=1, tiled=True)
    incoming = incoming.reshape(parts, slabs * rows, lanes)
    return tuple(incoming[part] for part in range(parts))


def columns_to_rows(real_part, imag_part, slabs, width, count):
    length = real_part.shape[0]
    rows = length // slabs
    outgoing = jnp.stack([real_part, imag_part]).reshape(2, slabs, rows, count * width)
    incoming = lax.all_to_all(outgoing, "slab", split_axis=1, concat_axis=1, tiled=True)
    incoming = incoming.reshape(2, slabs, rows, count, width)
    return jnp.transpose(incoming, (3, 0, 2, 1, 4)).reshape(count, 2, rows, slabs * width)


def along_columns(real_part, imag_part, plan, inverse):
    outer_tables, inner_tables, twiddle = plan
    outer_len = outer_tables[0].shape[0]
    inner_len = inner_tables[0].shape[0]
    length, lanes = real_part.shape

    def contract(tables, real_in, imag_in, axis):
        dims = (((0,), (axis,)), ((), ()))
        joined = jnp.concatenate(tables, axis=1)
        count = tables[0].shape[1]
        real_both = lax.dot_general(joined, real_in, dims, precision=highest)
        imag_both = lax.dot_general(joined, imag_in, dims, precision=highest)
        real_cos, real_sin = real_both[:count], real_both[count:]
        imag_cos, imag_sin = imag_both[:count], imag_both[count:]
        if inverse:
            return (real_cos - imag_sin, imag_cos + real_sin)
        return (real_cos + imag_sin, imag_cos - real_sin)

    if inverse:
        real_in = real_part.reshape(inner_len, outer_len, lanes)
        imag_in = imag_part.reshape(inner_len, outer_len, lanes)
        real_mid, imag_mid = contract(inner_tables, real_in, imag_in, 0)
        turn = (twiddle[0].T[:, :, None], twiddle[1].T[:, :, None])
        real_mid, imag_mid = twiddle_apply(real_mid, imag_mid, turn, True)
        real_out, imag_out = contract(outer_tables, real_mid, imag_mid, 1)
        scale = 1.0 / length
        return (real_out.reshape(length, lanes) * scale, imag_out.reshape(length, lanes) * scale)
    real_in = real_part.reshape(outer_len, inner_len, lanes)
    imag_in = imag_part.reshape(outer_len, inner_len, lanes)
    real_mid, imag_mid = contract(outer_tables, real_in, imag_in, 0)
    turn = (twiddle[0][:, :, None], twiddle[1][:, :, None])
    real_mid, imag_mid = twiddle_apply(real_mid, imag_mid, turn, False)
    real_out, imag_out = contract(inner_tables, real_mid, imag_mid, 1)
    return (real_out.reshape(length, lanes), imag_out.reshape(length, lanes))

def regroup_to_columns(values, width):
    depth, parts, rows, chunks, inner = values.shape
    per = inner // width
    lanes = depth * width
    inner_index = jnp.arange(inner, dtype=jnp.int32)
    out_index = jnp.arange(per * lanes, dtype=jnp.int32)
    out_group = out_index // lanes
    out_depth = (out_index // width) % depth
    out_cell = out_group * width + out_index % width
    depth_index = jnp.arange(depth, dtype=jnp.int32)
    permutation = (
        (depth_index[:, None, None] == out_depth[None, None, :])
        & (inner_index[None, :, None] == out_cell[None, None, :])
    ).astype(jnp.float32)
    moved = lax.dot_general(
        values, permutation, (((0, 4), (0, 1)), ((), ())), precision=highest
    )
    moved = moved.reshape(parts, rows, chunks, per, lanes)
    return jnp.transpose(moved, (2, 3, 0, 1, 4)).reshape(chunks * per, parts, rows, lanes)


def regroup_to_rows(real_part, imag_part, slabs, width, count):
    length, lanes = real_part.shape
    rows = length // slabs
    inner = 128
    per = inner // width
    chunks = slabs // per
    outgoing = jnp.transpose(
        jnp.stack([real_part, imag_part]).reshape(2, slabs, rows, lanes), (1, 0, 2, 3)
    )
    incoming = lax.all_to_all(outgoing, "slab", split_axis=0, concat_axis=0, tiled=True)
    incoming = incoming.reshape(chunks, per, 2, rows, lanes)
    lane_index = jnp.arange(lanes, dtype=jnp.int32)
    out_index = jnp.arange(count * inner, dtype=jnp.int32)
    out_depth = out_index // inner
    out_group = (out_index % inner) // width
    out_cell = out_index % width
    group_index = jnp.arange(per, dtype=jnp.int32)
    permutation = (
        (group_index[:, None, None] == out_group[None, None, :])
        & ((lane_index // width)[None, :, None] == out_depth[None, None, :])
        & ((lane_index % width)[None, :, None] == out_cell[None, None, :])
    ).astype(jnp.float32)
    moved = lax.dot_general(
        incoming, permutation, (((1, 4), (0, 1)), ((), ())), precision=highest
    )
    moved = moved.reshape(chunks, 2, rows, count, inner)
    return jnp.transpose(moved, (3, 1, 2, 0, 4))


def shards(volume, consensus, scaled_dual, amplitude, fresnel, ray_index, ray_weight):
    slice_cells = volume.shape[2]
    length = amplitude.shape[3]
    slabs = lax.axis_size("slab")
    width = length // slabs
    groups = lax.axis_size("group")
    inner_len = min(128, length)
    outer_len = length // inner_len
    outer_index = jnp.arange(outer_len, dtype=jnp.int32)
    inner_index = jnp.arange(inner_len, dtype=jnp.int32)
    twiddle_angle = (
        2.0 * math.pi / length * (outer_index[:, None] * inner_index[None, :]).astype(jnp.float32)
    )
    plan = (
        dft_tables(outer_len),
        dft_tables(inner_len),
        (jnp.cos(twiddle_angle), jnp.sin(twiddle_angle)),
    )
    cell_ids = jnp.arange(slice_cells, dtype=jnp.int32)
    projector = jnp.zeros((length, slice_cells), jnp.float32)
    for tap_number in range(ray_index.shape[1]):
        hit = (ray_index[0, tap_number][:, None] == cell_ids[None, :]).astype(jnp.float32)
        projector = projector + ray_weight[0, tap_number][:, None] * hit
    thickness = lax.dot_general(volume[0], projector, (((1,), (1,)), ((), ())), precision=highest)
    wavefront = jnp.stack([jnp.cos(thickness), jnp.sin(thickness)])
    row_spectrum = along_last(wavefront, plan, False)
    position = jnp.arange(length, dtype=jnp.int32)
    row_freq = position // inner_len + outer_len * (position % inner_len)
    centered_u = jnp.where(row_freq < length // 2, row_freq, row_freq - length)
    phase_u = (
        -math.pi * fresnel[:, None] * (centered_u * centered_u).astype(jnp.float32)[None, :]
        / HOLOGRAM
    )
    row_kernel_real = jnp.cos(phase_u)[:, None, :]
    row_kernel_imag = jnp.sin(phase_u)[:, None, :]
    u_fields = along_last(
        jnp.stack(
            [
                row_kernel_real * row_spectrum[0] - row_kernel_imag * row_spectrum[1],
                row_kernel_real * row_spectrum[1] + row_kernel_imag * row_spectrum[0],
            ],
            axis=1,
        ),
        plan,
        True,
        split=True,
    )
    measured = amplitude[0].reshape((DISTANCES, 1, amplitude.shape[2]) + u_fields.shape[-2:])
    packed = jnp.concatenate(
        [regroup_to_columns(u_fields, width), regroup_to_columns(measured, width)], axis=1
    )
    incoming = lax.all_to_all(packed, "slab", split_axis=0, concat_axis=0, tiled=True)
    column_real, column_imag, column_amplitude = (
        incoming[:, part].reshape(length, DISTANCES * width) for part in range(3)
    )
    centered_z = jnp.where(position < length // 2, position, position - length)
    phase_z = (
        -math.pi * fresnel[None, :, None]
        * (centered_z * centered_z).astype(jnp.float32)[:, None, None]
        / HOLOGRAM
    )
    lanes = DISTANCES * width
    phase_z = jnp.broadcast_to(phase_z, (length, DISTANCES, width)).reshape(length, lanes)
    kernel_real = jnp.cos(phase_z)
    kernel_imag = jnp.sin(phase_z)
    spectrum_real, spectrum_imag = along_columns(column_real, column_imag, plan, False)
    field_real, field_imag = along_columns(
        kernel_real * spectrum_real - kernel_imag * spectrum_imag,
        kernel_real * spectrum_imag + kernel_imag * spectrum_real,
        plan,
        True,
    )
    magnitude = jnp.sqrt(field_real * field_real + field_imag * field_imag)
    factor = column_amplitude / jnp.maximum(magnitude, mod_floor)
    moduli_real, moduli_imag = along_columns(field_real * factor, field_imag * factor, plan, False)
    turned_real, turned_imag = along_columns(
        kernel_real * moduli_real + kernel_imag * moduli_imag,
        kernel_real * moduli_imag - kernel_imag * moduli_real,
        plan,
        True,
    )
    row_moduli = along_last(
        regroup_to_rows(turned_real, turned_imag, slabs, width, DISTANCES),
        plan,
        False,
        split_in=True,
    )
    total_real = jnp.sum(
        row_kernel_real * row_moduli[:, 0] + row_kernel_imag * row_moduli[:, 1],
        axis=0,
    )
    total_imag = jnp.sum(
        row_kernel_real * row_moduli[:, 1] - row_kernel_imag * row_moduli[:, 0],
        axis=0,
    )
    back = along_last(jnp.stack([total_real, total_imag]) / DISTANCES, plan, True)
    gradient = jnp.cos(thickness) * back[1] - jnp.sin(thickness) * back[0]
    bprojected = jnp.matmul(gradient, projector, precision=highest)
    volume_next = volume[0] + step_size * (
        bprojected - penalty * (volume[0] - consensus + scaled_dual[0])
    )
    combined = volume_next + scaled_dual[0]
    total = combined
    step = 1
    while step < groups:
        pairs = [(index, index ^ step) for index in range(groups)]
        total = total + lax.ppermute(total, "group", pairs)
        step *= 2
    consensus_next = total / groups
    dual_next = scaled_dual[0] + volume_next - consensus_next
    return (volume_next[None], consensus_next, dual_next[None])


def solution(mesh):
    placed = (
        P("group", "slab", None),
        P("slab", None),
        P("group", "slab", None),
        P("group", None, "slab", None),
        P(),
        P("group", None, None),
        P("group", None, None),
    )
    return jax.shard_map(
        shards,
        mesh=mesh,
        in_specs=placed,
        out_specs=(P("group", "slab", None), P("slab", None), P("group", "slab", None)),
        check_vma=False,
    )
```

```python
import math

import jax
import jax.numpy as jnp
from jax import lax
from jax.sharding import PartitionSpec as P

HOLOGRAM = 1024
DISTANCES = 4


step_size = 0.5
penalty = 0.5
mod_floor = 0.25
highest = lax.Precision.HIGHEST


def dft_tables(count):
    index = jnp.arange(count, dtype=jnp.int32)
    angle = 2.0 * math.pi / count * (index[:, None] * index[None, :] % count).astype(jnp.float32)
    return (jnp.cos(angle), jnp.sin(angle))


def complex_contract(real_part, imag_part, tables, form, inverse):
    joined = jnp.concatenate(tables, axis=1)
    count = tables[0].shape[1]
    out_spec = form.split("->")[1]
    axis = out_spec.index(form.split(",")[1][1]) - len(out_spec)
    both = jnp.einsum(form, jnp.stack([real_part, imag_part]), joined, precision=highest)
    real_both, imag_both = both[0], both[1]
    real_cos = lax.slice_in_dim(real_both, 0, count, axis=axis)
    real_sin = lax.slice_in_dim(real_both, count, 2 * count, axis=axis)
    imag_cos = lax.slice_in_dim(imag_both, 0, count, axis=axis)
    imag_sin = lax.slice_in_dim(imag_both, count, 2 * count, axis=axis)
    if inverse:
        return (real_cos - imag_sin, imag_cos + real_sin)
    return (real_cos + imag_sin, imag_cos - real_sin)


def twiddle_apply(real_part, imag_part, twiddle, inverse):
    twiddle_cos, twiddle_sin = twiddle
    if inverse:
        return (
            real_part * twiddle_cos - imag_part * twiddle_sin,
            imag_part * twiddle_cos + real_part * twiddle_sin,
        )
    return (
        real_part * twiddle_cos + imag_part * twiddle_sin,
        imag_part * twiddle_cos - real_part * twiddle_sin,
    )


def along_last(values, plan, inverse, split=False, split_in=False):
    outer_tables, inner_tables, twiddle = plan
    outer_len = outer_tables[0].shape[0]
    inner_len = inner_tables[0].shape[0]
    if split_in:
        real_part = values[..., 0, :, :, :]
        imag_part = values[..., 1, :, :, :]
        shape = real_part.shape[:-2] + (outer_len * inner_len,)
    else:
        real_part = values[..., 0, :, :]
        imag_part = values[..., 1, :, :]
        shape = real_part.shape
    length = shape[-1]
    real_part = real_part.reshape(shape[:-1] + (outer_len, inner_len))
    imag_part = imag_part.reshape(shape[:-1] + (outer_len, inner_len))
    outer_form = "...ab,ak->...kb"
    inner_form = "...ab,bl->...al"
    if inverse:
        real_part, imag_part = complex_contract(
            real_part, imag_part, inner_tables, inner_form, True
        )
        real_part, imag_part = twiddle_apply(real_part, imag_part, twiddle, True)
        real_part, imag_part = complex_contract(
            real_part, imag_part, outer_tables, outer_form, True
        )
    else:
        real_part, imag_part = complex_contract(
            real_part, imag_part, outer_tables, outer_form, False
        )
        real_part, imag_part = twiddle_apply(real_part, imag_part, twiddle, False)
        real_part, imag_part = complex_contract(
            real_part, imag_part, inner_tables, inner_form, False
        )
    if split:
        result = jnp.stack([real_part, imag_part], axis=-4)
    else:
        result = jnp.stack([real_part.reshape(shape), imag_part.reshape(shape)], axis=-3)
    if inverse:
        return result * (1.0 / length)
    return result


def along_first(values, plan, inverse):
    outer_tables, inner_tables, twiddle = plan
    outer_len = outer_tables[0].shape[0]
    inner_len = inner_tables[0].shape[0]
    real_part = values[..., 0, :, :]
    imag_part = values[..., 1, :, :]
    shape = real_part.shape
    length = shape[-2]
    split_shape = shape[:-2] + (outer_len, inner_len, shape[-1])
    real_part = real_part.reshape(split_shape)
    imag_part = imag_part.reshape(split_shape)
    twiddle_cols = (twiddle[0][:, :, None], twiddle[1][:, :, None])
    outer_form = "...abw,ak->...kbw"
    inner_form = "...abw,bl->...alw"
    if inverse:
        real_part, imag_part = complex_contract(
            real_part, imag_part, inner_tables, inner_form, True
        )
        real_part, imag_part = twiddle_apply(real_part, imag_part, twiddle_cols, True)
        real_part, imag_part = complex_contract(
            real_part, imag_part, outer_tables, outer_form, True
        )
    else:
        real_part, imag_part = complex_contract(
            real_part, imag_part, outer_tables, outer_form, False
        )
        real_part, imag_part = twiddle_apply(real_part, imag_part, twiddle_cols, False)
        real_part, imag_part = complex_contract(
            real_part, imag_part, inner_tables, inner_form, False
        )
    result = jnp.stack([real_part.reshape(shape), imag_part.reshape(shape)], axis=-3)
    if inverse:
        return result * (1.0 / length)
    return result


def rows_to_columns(values, slabs, width):
    lead = values.shape[:-3]
    rank = len(lead)
    rows = values.shape[-2]
    parts = values.shape[-3]
    blocks = values.reshape(lead + (parts, rows, slabs, width))
    order = (rank, rank + 2, rank + 1) + tuple(range(rank)) + (rank + 3,)
    lanes = width
    for size in lead:
        lanes *= size
    outgoing = jnp.transpose(blocks, order).reshape(parts, slabs, rows, lanes)
    incoming = lax.all_to_all(outgoing, "slab", split_axis=1, concat_axis=1, tiled=True)
    incoming = incoming.reshape(parts, slabs * rows, lanes)
    return tuple(incoming[part] for part in range(parts))


def columns_to_rows(real_part, imag_part, slabs, width, count):
    length = real_part.shape[0]
    rows = length // slabs
    outgoing = jnp.stack([real_part, imag_part]).reshape(2, slabs, rows, count * width)
    incoming = lax.all_to_all(outgoing, "slab", split_axis=1, concat_axis=1, tiled=True)
    incoming = incoming.reshape(2, slabs, rows, count, width)
    return jnp.transpose(incoming, (3, 0, 2, 1, 4)).reshape(count, 2, rows, slabs * width)


def along_columns(real_part, imag_part, plan, inverse):
    outer_tables, inner_tables, twiddle = plan
    outer_len = outer_tables[0].shape[0]
    inner_len = inner_tables[0].shape[0]
    length, lanes = real_part.shape

    def contract(tables, real_in, imag_in, axis):
        joined = jnp.concatenate(tables, axis=1)
        count = tables[0].shape[1]
        stacked_dims = (((0,), (axis + 1,)), ((), ()))
        both = lax.dot_general(
            joined, jnp.stack([real_in, imag_in]), stacked_dims, precision=highest
        )
        real_both, imag_both = both[:, 0], both[:, 1]
        real_cos, real_sin = real_both[:count], real_both[count:]
        imag_cos, imag_sin = imag_both[:count], imag_both[count:]
        if inverse:
            return (real_cos - imag_sin, imag_cos + real_sin)
        return (real_cos + imag_sin, imag_cos - real_sin)

    if inverse:
        real_in = real_part.reshape(inner_len, outer_len, lanes)
        imag_in = imag_part.reshape(inner_len, outer_len, lanes)
        real_mid, imag_mid = contract(inner_tables, real_in, imag_in, 0)
        turn = (twiddle[0].T[:, :, None], twiddle[1].T[:, :, None])
        real_mid, imag_mid = twiddle_apply(real_mid, imag_mid, turn, True)
        real_out, imag_out = contract(outer_tables, real_mid, imag_mid, 1)
        scale = 1.0 / length
        return (real_out.reshape(length, lanes) * scale, imag_out.reshape(length, lanes) * scale)
    real_in = real_part.reshape(outer_len, inner_len, lanes)
    imag_in = imag_part.reshape(outer_len, inner_len, lanes)
    real_mid, imag_mid = contract(outer_tables, real_in, imag_in, 0)
    turn = (twiddle[0][:, :, None], twiddle[1][:, :, None])
    real_mid, imag_mid = twiddle_apply(real_mid, imag_mid, turn, False)
    real_out, imag_out = contract(inner_tables, real_mid, imag_mid, 1)
    return (real_out.reshape(length, lanes), imag_out.reshape(length, lanes))

def regroup_to_columns(values, width):
    depth, parts, rows, chunks, inner = values.shape
    per = inner // width
    lanes = depth * width
    inner_index = jnp.arange(inner, dtype=jnp.int32)
    out_index = jnp.arange(per * lanes, dtype=jnp.int32)
    out_group = out_index // lanes
    out_depth = (out_index // width) % depth
    out_cell = out_group * width + out_index % width
    depth_index = jnp.arange(depth, dtype=jnp.int32)
    permutation = (
        (depth_index[:, None, None] == out_depth[None, None, :])
        & (inner_index[None, :, None] == out_cell[None, None, :])
    ).astype(jnp.float32)
    moved = lax.dot_general(
        values, permutation, (((0, 4), (0, 1)), ((), ())), precision=highest
    )
    moved = moved.reshape(parts, rows, chunks, per, lanes)
    return jnp.transpose(moved, (2, 3, 0, 1, 4)).reshape(chunks * per, parts, rows, lanes)


def regroup_to_rows(real_part, imag_part, slabs, width, count):
    length, lanes = real_part.shape
    rows = length // slabs
    inner = 128
    per = inner // width
    chunks = slabs // per
    outgoing = jnp.transpose(
        jnp.stack([real_part, imag_part]).reshape(2, slabs, rows, lanes), (1, 0, 2, 3)
    )
    incoming = lax.all_to_all(outgoing, "slab", split_axis=0, concat_axis=0, tiled=True)
    incoming = incoming.reshape(chunks, per, 2, rows, lanes)
    lane_index = jnp.arange(lanes, dtype=jnp.int32)
    out_index = jnp.arange(count * inner, dtype=jnp.int32)
    out_depth = out_index // inner
    out_group = (out_index % inner) // width
    out_cell = out_index % width
    group_index = jnp.arange(per, dtype=jnp.int32)
    permutation = (
        (group_index[:, None, None] == out_group[None, None, :])
        & ((lane_index // width)[None, :, None] == out_depth[None, None, :])
        & ((lane_index % width)[None, :, None] == out_cell[None, None, :])
    ).astype(jnp.float32)
    moved = lax.dot_general(
        incoming, permutation, (((1, 4), (0, 1)), ((), ())), precision=highest
    )
    moved = moved.reshape(chunks, 2, rows, count, inner)
    return jnp.transpose(moved, (3, 1, 2, 0, 4))


def shards(volume, consensus, scaled_dual, amplitude, fresnel, ray_index, ray_weight):
    slice_cells = volume.shape[2]
    length = amplitude.shape[3]
    slabs = lax.axis_size("slab")
    width = length // slabs
    groups = lax.axis_size("group")
    inner_len = min(128, length)
    outer_len = length // inner_len
    outer_index = jnp.arange(outer_len, dtype=jnp.int32)
    inner_index = jnp.arange(inner_len, dtype=jnp.int32)
    twiddle_angle = (
        2.0 * math.pi / length * (outer_index[:, None] * inner_index[None, :]).astype(jnp.float32)
    )
    plan = (
        dft_tables(outer_len),
        dft_tables(inner_len),
        (jnp.cos(twiddle_angle), jnp.sin(twiddle_angle)),
    )
    cell_ids = jnp.arange(slice_cells, dtype=jnp.int32)
    projector = jnp.zeros((length, slice_cells), jnp.float32)
    for tap_number in range(ray_index.shape[1]):
        hit = (ray_index[0, tap_number][:, None] == cell_ids[None, :]).astype(jnp.float32)
        projector = projector + ray_weight[0, tap_number][:, None] * hit
    thickness = lax.dot_general(volume[0], projector, (((1,), (1,)), ((), ())), precision=highest)
    wavefront = jnp.stack([jnp.cos(thickness), jnp.sin(thickness)])
    row_spectrum = along_last(wavefront, plan, False)
    position = jnp.arange(length, dtype=jnp.int32)
    row_freq = position // inner_len + outer_len * (position % inner_len)
    centered_u = jnp.where(row_freq < length // 2, row_freq, row_freq - length)
    phase_u = (
        -math.pi * fresnel[:, None] * (centered_u * centered_u).astype(jnp.float32)[None, :]
        / HOLOGRAM
    )
    row_kernel_real = jnp.cos(phase_u)[:, None, :]
    row_kernel_imag = jnp.sin(phase_u)[:, None, :]
    u_fields = along_last(
        jnp.stack(
            [
                row_kernel_real * row_spectrum[0] - row_kernel_imag * row_spectrum[1],
                row_kernel_real * row_spectrum[1] + row_kernel_imag * row_spectrum[0],
            ],
            axis=1,
        ),
        plan,
        True,
        split=True,
    )
    measured = amplitude[0].reshape((DISTANCES, 1, amplitude.shape[2]) + u_fields.shape[-2:])
    packed = jnp.concatenate(
        [regroup_to_columns(u_fields, width), regroup_to_columns(measured, width)], axis=1
    )
    incoming = lax.all_to_all(packed, "slab", split_axis=0, concat_axis=0, tiled=True)
    column_real, column_imag, column_amplitude = (
        incoming[:, part].reshape(length, DISTANCES * width) for part in range(3)
    )
    centered_z = jnp.where(position < length // 2, position, position - length)
    phase_z = (
        -math.pi * fresnel[None, :, None]
        * (centered_z * centered_z).astype(jnp.float32)[:, None, None]
        / HOLOGRAM
    )
    lanes = DISTANCES * width
    phase_z = jnp.broadcast_to(phase_z, (length, DISTANCES, width)).reshape(length, lanes)
    kernel_real = jnp.cos(phase_z)
    kernel_imag = jnp.sin(phase_z)
    spectrum_real, spectrum_imag = along_columns(column_real, column_imag, plan, False)
    field_real, field_imag = along_columns(
        kernel_real * spectrum_real - kernel_imag * spectrum_imag,
        kernel_real * spectrum_imag + kernel_imag * spectrum_real,
        plan,
        True,
    )
    magnitude = jnp.sqrt(field_real * field_real + field_imag * field_imag)
    factor = column_amplitude / jnp.maximum(magnitude, mod_floor)
    moduli_real, moduli_imag = along_columns(field_real * factor, field_imag * factor, plan, False)
    turned_real, turned_imag = along_columns(
        kernel_real * moduli_real + kernel_imag * moduli_imag,
        kernel_real * moduli_imag - kernel_imag * moduli_real,
        plan,
        True,
    )
    row_moduli = along_last(
        regroup_to_rows(turned_real, turned_imag, slabs, width, DISTANCES),
        plan,
        False,
        split_in=True,
    )
    total_real = jnp.sum(
        row_kernel_real * row_moduli[:, 0] + row_kernel_imag * row_moduli[:, 1],
        axis=0,
    )
    total_imag = jnp.sum(
        row_kernel_real * row_moduli[:, 1] - row_kernel_imag * row_moduli[:, 0],
        axis=0,
    )
    back = along_last(jnp.stack([total_real, total_imag]) / DISTANCES, plan, True)
    gradient = jnp.cos(thickness) * back[1] - jnp.sin(thickness) * back[0]
    bprojected = jnp.matmul(gradient, projector, precision=highest)
    volume_next = volume[0] + step_size * (
        bprojected - penalty * (volume[0] - consensus + scaled_dual[0])
    )
    combined = volume_next + scaled_dual[0]
    total = combined
    step = 1
    while step < groups:
        pairs = [(index, index ^ step) for index in range(groups)]
        total = total + lax.ppermute(total, "group", pairs)
        step *= 2
    consensus_next = total / groups
    dual_next = scaled_dual[0] + volume_next - consensus_next
    return (volume_next[None], consensus_next, dual_next[None])


def solution(mesh):
    placed = (
        P("group", "slab", None),
        P("slab", None),
        P("group", "slab", None),
        P("group", None, "slab", None),
        P(),
        P("group", None, None),
        P("group", None, None),
    )
    return jax.shard_map(
        shards,
        mesh=mesh,
        in_specs=placed,
        out_specs=(P("group", "slab", None), P("slab", None), P("group", "slab", None)),
        check_vma=False,
    )
```

```python
import math

import jax
import jax.numpy as jnp
from jax import lax
from jax.sharding import PartitionSpec as P

HOLOGRAM = 1024
DISTANCES = 4


step_size = 0.5
penalty = 0.5
mod_floor = 0.25
highest = lax.Precision.HIGHEST


def dft_tables(count):
    index = jnp.arange(count, dtype=jnp.int32)
    angle = 2.0 * math.pi / count * (index[:, None] * index[None, :] % count).astype(jnp.float32)
    return (jnp.cos(angle), jnp.sin(angle))


def complex_contract(real_part, imag_part, tables, form, inverse):
    joined = jnp.concatenate(tables, axis=1)
    count = tables[0].shape[1]
    out_spec = form.split("->")[1]
    axis = out_spec.index(form.split(",")[1][1]) - len(out_spec)
    real_both = jnp.einsum(form, real_part, joined, precision=highest)
    imag_both = jnp.einsum(form, imag_part, joined, precision=highest)
    real_cos = lax.slice_in_dim(real_both, 0, count, axis=axis)
    real_sin = lax.slice_in_dim(real_both, count, 2 * count, axis=axis)
    imag_cos = lax.slice_in_dim(imag_both, 0, count, axis=axis)
    imag_sin = lax.slice_in_dim(imag_both, count, 2 * count, axis=axis)
    if inverse:
        return (real_cos - imag_sin, imag_cos + real_sin)
    return (real_cos + imag_sin, imag_cos - real_sin)


def twiddle_apply(real_part, imag_part, twiddle, inverse):
    twiddle_cos, twiddle_sin = twiddle
    if inverse:
        return (
            real_part * twiddle_cos - imag_part * twiddle_sin,
            imag_part * twiddle_cos + real_part * twiddle_sin,
        )
    return (
        real_part * twiddle_cos + imag_part * twiddle_sin,
        imag_part * twiddle_cos - real_part * twiddle_sin,
    )


def along_last(values, plan, inverse, split=False, split_in=False):
    outer_tables, inner_tables, twiddle = plan
    outer_len = outer_tables[0].shape[0]
    inner_len = inner_tables[0].shape[0]
    if split_in:
        real_part = values[..., 0, :, :, :]
        imag_part = values[..., 1, :, :, :]
        shape = real_part.shape[:-2] + (outer_len * inner_len,)
    else:
        real_part = values[..., 0, :, :]
        imag_part = values[..., 1, :, :]
        shape = real_part.shape
    length = shape[-1]
    real_part = real_part.reshape(shape[:-1] + (outer_len, inner_len))
    imag_part = imag_part.reshape(shape[:-1] + (outer_len, inner_len))
    outer_form = "...ab,ak->...kb"
    inner_form = "...ab,bl->...al"
    if inverse:
        real_part, imag_part = complex_contract(
            real_part, imag_part, inner_tables, inner_form, True
        )
        real_part, imag_part = twiddle_apply(real_part, imag_part, twiddle, True)
        real_part, imag_part = complex_contract(
            real_part, imag_part, outer_tables, outer_form, True
        )
    else:
        real_part, imag_part = complex_contract(
            real_part, imag_part, outer_tables, outer_form, False
        )
        real_part, imag_part = twiddle_apply(real_part, imag_part, twiddle, False)
        real_part, imag_part = complex_contract(
            real_part, imag_part, inner_tables, inner_form, False
        )
    if split:
        result = jnp.stack([real_part, imag_part], axis=-4)
    else:
        result = jnp.stack([real_part.reshape(shape), imag_part.reshape(shape)], axis=-3)
    if inverse:
        return result * (1.0 / length)
    return result


def along_first(values, plan, inverse):
    outer_tables, inner_tables, twiddle = plan
    outer_len = outer_tables[0].shape[0]
    inner_len = inner_tables[0].shape[0]
    real_part = values[..., 0, :, :]
    imag_part = values[..., 1, :, :]
    shape = real_part.shape
    length = shape[-2]
    split_shape = shape[:-2] + (outer_len, inner_len, shape[-1])
    real_part = real_part.reshape(split_shape)
    imag_part = imag_part.reshape(split_shape)
    twiddle_cols = (twiddle[0][:, :, None], twiddle[1][:, :, None])
    outer_form = "...abw,ak->...kbw"
    inner_form = "...abw,bl->...alw"
    if inverse:
        real_part, imag_part = complex_contract(
            real_part, imag_part, inner_tables, inner_form, True
        )
        real_part, imag_part = twiddle_apply(real_part, imag_part, twiddle_cols, True)
        real_part, imag_part = complex_contract(
            real_part, imag_part, outer_tables, outer_form, True
        )
    else:
        real_part, imag_part = complex_contract(
            real_part, imag_part, outer_tables, outer_form, False
        )
        real_part, imag_part = twiddle_apply(real_part, imag_part, twiddle_cols, False)
        real_part, imag_part = complex_contract(
            real_part, imag_part, inner_tables, inner_form, False
        )
    result = jnp.stack([real_part.reshape(shape), imag_part.reshape(shape)], axis=-3)
    if inverse:
        return result * (1.0 / length)
    return result


def rows_to_columns(values, slabs, width):
    lead = values.shape[:-3]
    rank = len(lead)
    rows = values.shape[-2]
    parts = values.shape[-3]
    blocks = values.reshape(lead + (parts, rows, slabs, width))
    order = (rank, rank + 2, rank + 1) + tuple(range(rank)) + (rank + 3,)
    lanes = width
    for size in lead:
        lanes *= size
    outgoing = jnp.transpose(blocks, order).reshape(parts, slabs, rows, lanes)
    incoming = lax.all_to_all(outgoing, "slab", split_axis=1, concat_axis=1, tiled=True)
    incoming = incoming.reshape(parts, slabs * rows, lanes)
    return tuple(incoming[part] for part in range(parts))


def columns_to_rows(real_part, imag_part, slabs, width, count):
    length = real_part.shape[0]
    rows = length // slabs
    outgoing = jnp.stack([real_part, imag_part]).reshape(2, slabs, rows, count * width)
    incoming = lax.all_to_all(outgoing, "slab", split_axis=1, concat_axis=1, tiled=True)
    incoming = incoming.reshape(2, slabs, rows, count, width)
    return jnp.transpose(incoming, (3, 0, 2, 1, 4)).reshape(count, 2, rows, slabs * width)


def along_columns(real_part, imag_part, plan, inverse):
    outer_tables, inner_tables, twiddle = plan
    outer_len = outer_tables[0].shape[0]
    inner_len = inner_tables[0].shape[0]
    length, lanes = real_part.shape

    def contract(tables, real_in, imag_in, axis):
        joined = jnp.concatenate(tables, axis=1)
        count = tables[0].shape[1]
        stacked_dims = (((0,), (axis + 1,)), ((), ()))
        both = lax.dot_general(
            joined, jnp.stack([real_in, imag_in]), stacked_dims, precision=highest
        )
        real_both, imag_both = both[:, 0], both[:, 1]
        real_cos, real_sin = real_both[:count], real_both[count:]
        imag_cos, imag_sin = imag_both[:count], imag_both[count:]
        if inverse:
            return (real_cos - imag_sin, imag_cos + real_sin)
        return (real_cos + imag_sin, imag_cos - real_sin)

    if inverse:
        real_in = real_part.reshape(inner_len, outer_len, lanes)
        imag_in = imag_part.reshape(inner_len, outer_len, lanes)
        real_mid, imag_mid = contract(inner_tables, real_in, imag_in, 0)
        turn = (twiddle[0].T[:, :, None], twiddle[1].T[:, :, None])
        real_mid, imag_mid = twiddle_apply(real_mid, imag_mid, turn, True)
        real_out, imag_out = contract(outer_tables, real_mid, imag_mid, 1)
        scale = 1.0 / length
        return (real_out.reshape(length, lanes) * scale, imag_out.reshape(length, lanes) * scale)
    real_in = real_part.reshape(outer_len, inner_len, lanes)
    imag_in = imag_part.reshape(outer_len, inner_len, lanes)
    real_mid, imag_mid = contract(outer_tables, real_in, imag_in, 0)
    turn = (twiddle[0][:, :, None], twiddle[1][:, :, None])
    real_mid, imag_mid = twiddle_apply(real_mid, imag_mid, turn, False)
    real_out, imag_out = contract(inner_tables, real_mid, imag_mid, 1)
    return (real_out.reshape(length, lanes), imag_out.reshape(length, lanes))

def regroup_to_columns(values, width):
    depth, parts, rows, chunks, inner = values.shape
    per = inner // width
    lanes = depth * width
    inner_index = jnp.arange(inner, dtype=jnp.int32)
    out_index = jnp.arange(per * lanes, dtype=jnp.int32)
    out_group = out_index // lanes
    out_depth = (out_index // width) % depth
    out_cell = out_group * width + out_index % width
    depth_index = jnp.arange(depth, dtype=jnp.int32)
    permutation = (
        (depth_index[:, None, None] == out_depth[None, None, :])
        & (inner_index[None, :, None] == out_cell[None, None, :])
    ).astype(jnp.float32)
    moved = lax.dot_general(
        values, permutation, (((0, 4), (0, 1)), ((), ())), precision=highest
    )
    moved = moved.reshape(parts, rows, chunks, per, lanes)
    return jnp.transpose(moved, (2, 3, 0, 1, 4)).reshape(chunks * per, parts, rows, lanes)


def regroup_to_rows(real_part, imag_part, slabs, width, count):
    length, lanes = real_part.shape
    rows = length // slabs
    inner = 128
    per = inner // width
    chunks = slabs // per
    outgoing = jnp.transpose(
        jnp.stack([real_part, imag_part]).reshape(2, slabs, rows, lanes), (1, 0, 2, 3)
    )
    incoming = lax.all_to_all(outgoing, "slab", split_axis=0, concat_axis=0, tiled=True)
    incoming = incoming.reshape(chunks, per, 2, rows, lanes)
    lane_index = jnp.arange(lanes, dtype=jnp.int32)
    out_index = jnp.arange(count * inner, dtype=jnp.int32)
    out_depth = out_index // inner
    out_group = (out_index % inner) // width
    out_cell = out_index % width
    group_index = jnp.arange(per, dtype=jnp.int32)
    permutation = (
        (group_index[:, None, None] == out_group[None, None, :])
        & ((lane_index // width)[None, :, None] == out_depth[None, None, :])
        & ((lane_index % width)[None, :, None] == out_cell[None, None, :])
    ).astype(jnp.float32)
    moved = lax.dot_general(
        incoming, permutation, (((1, 4), (0, 1)), ((), ())), precision=highest
    )
    moved = moved.reshape(chunks, 2, rows, count, inner)
    return jnp.transpose(moved, (3, 1, 2, 0, 4))


def shards(volume, consensus, scaled_dual, amplitude, fresnel, ray_index, ray_weight):
    slice_cells = volume.shape[2]
    length = amplitude.shape[3]
    slabs = lax.axis_size("slab")
    width = length // slabs
    groups = lax.axis_size("group")
    inner_len = min(128, length)
    outer_len = length // inner_len
    outer_index = jnp.arange(outer_len, dtype=jnp.int32)
    inner_index = jnp.arange(inner_len, dtype=jnp.int32)
    twiddle_angle = (
        2.0 * math.pi / length * (outer_index[:, None] * inner_index[None, :]).astype(jnp.float32)
    )
    plan = (
        dft_tables(outer_len),
        dft_tables(inner_len),
        (jnp.cos(twiddle_angle), jnp.sin(twiddle_angle)),
    )
    cell_ids = jnp.arange(slice_cells, dtype=jnp.int32)
    projector = jnp.zeros((length, slice_cells), jnp.float32)
    for tap_number in range(ray_index.shape[1]):
        hit = (ray_index[0, tap_number][:, None] == cell_ids[None, :]).astype(jnp.float32)
        projector = projector + ray_weight[0, tap_number][:, None] * hit
    thickness = lax.dot_general(volume[0], projector, (((1,), (1,)), ((), ())), precision=highest)
    wavefront = jnp.stack([jnp.cos(thickness), jnp.sin(thickness)])
    row_spectrum = along_last(wavefront, plan, False)
    position = jnp.arange(length, dtype=jnp.int32)
    row_freq = position // inner_len + outer_len * (position % inner_len)
    centered_u = jnp.where(row_freq < length // 2, row_freq, row_freq - length)
    phase_u = (
        -math.pi * fresnel[:, None] * (centered_u * centered_u).astype(jnp.float32)[None, :]
        / HOLOGRAM
    )
    row_kernel_real = jnp.cos(phase_u)[:, None, :]
    row_kernel_imag = jnp.sin(phase_u)[:, None, :]
    u_fields = along_last(
        jnp.stack(
            [
                row_kernel_real * row_spectrum[0] - row_kernel_imag * row_spectrum[1],
                row_kernel_real * row_spectrum[1] + row_kernel_imag * row_spectrum[0],
            ],
            axis=1,
        ),
        plan,
        True,
        split=True,
    )
    measured = amplitude[0].reshape((DISTANCES, 1, amplitude.shape[2]) + u_fields.shape[-2:])
    packed = jnp.concatenate(
        [regroup_to_columns(u_fields, width), regroup_to_columns(measured, width)], axis=1
    )
    incoming = lax.all_to_all(packed, "slab", split_axis=0, concat_axis=0, tiled=True)
    column_real, column_imag, column_amplitude = (
        incoming[:, part].reshape(length, DISTANCES * width) for part in range(3)
    )
    centered_z = jnp.where(position < length // 2, position, position - length)
    phase_z = (
        -math.pi * fresnel[None, :, None]
        * (centered_z * centered_z).astype(jnp.float32)[:, None, None]
        / HOLOGRAM
    )
    lanes = DISTANCES * width
    phase_z = jnp.broadcast_to(phase_z, (length, DISTANCES, width)).reshape(length, lanes)
    kernel_real = jnp.cos(phase_z)
    kernel_imag = jnp.sin(phase_z)
    spectrum_real, spectrum_imag = along_columns(column_real, column_imag, plan, False)
    field_real, field_imag = along_columns(
        kernel_real * spectrum_real - kernel_imag * spectrum_imag,
        kernel_real * spectrum_imag + kernel_imag * spectrum_real,
        plan,
        True,
    )
    magnitude = jnp.sqrt(field_real * field_real + field_imag * field_imag)
    factor = column_amplitude / jnp.maximum(magnitude, mod_floor)
    moduli_real, moduli_imag = along_columns(field_real * factor, field_imag * factor, plan, False)
    turned_real, turned_imag = along_columns(
        kernel_real * moduli_real + kernel_imag * moduli_imag,
        kernel_real * moduli_imag - kernel_imag * moduli_real,
        plan,
        True,
    )
    row_moduli = along_last(
        regroup_to_rows(turned_real, turned_imag, slabs, width, DISTANCES),
        plan,
        False,
        split_in=True,
    )
    total_real = jnp.sum(
        row_kernel_real * row_moduli[:, 0] + row_kernel_imag * row_moduli[:, 1],
        axis=0,
    )
    total_imag = jnp.sum(
        row_kernel_real * row_moduli[:, 1] - row_kernel_imag * row_moduli[:, 0],
        axis=0,
    )
    back = along_last(jnp.stack([total_real, total_imag]) / DISTANCES, plan, True)
    gradient = jnp.cos(thickness) * back[1] - jnp.sin(thickness) * back[0]
    bprojected = jnp.matmul(gradient, projector, precision=highest)
    volume_next = volume[0] + step_size * (
        bprojected - penalty * (volume[0] - consensus + scaled_dual[0])
    )
    combined = volume_next + scaled_dual[0]
    total = combined
    step = 1
    while step < groups:
        pairs = [(index, index ^ step) for index in range(groups)]
        total = total + lax.ppermute(total, "group", pairs)
        step *= 2
    consensus_next = total / groups
    dual_next = scaled_dual[0] + volume_next - consensus_next
    return (volume_next[None], consensus_next, dual_next[None])


def solution(mesh):
    placed = (
        P("group", "slab", None),
        P("slab", None),
        P("group", "slab", None),
        P("group", None, "slab", None),
        P(),
        P("group", None, None),
        P("group", None, None),
    )
    return jax.shard_map(
        shards,
        mesh=mesh,
        in_specs=placed,
        out_specs=(P("group", "slab", None), P("slab", None), P("group", "slab", None)),
        check_vma=False,
    )
```

```python
import math

import jax
import jax.numpy as jnp
from jax import lax
from jax.sharding import PartitionSpec as P

HOLOGRAM = 1024
DISTANCES = 4


step_size = 0.5
penalty = 0.5
mod_floor = 0.25
highest = lax.Precision.HIGHEST


def dft_tables(count):
    index = jnp.arange(count, dtype=jnp.int32)
    angle = 2.0 * math.pi / count * (index[:, None] * index[None, :] % count).astype(jnp.float32)
    return (jnp.cos(angle), jnp.sin(angle))


def complex_contract(real_part, imag_part, tables, form, inverse):
    joined = jnp.concatenate(tables, axis=1)
    count = tables[0].shape[1]
    out_spec = form.split("->")[1]
    axis = out_spec.index(form.split(",")[1][1]) - len(out_spec)
    if axis == -1:
        both = jnp.einsum(form, jnp.stack([real_part, imag_part]), joined, precision=highest)
        real_both, imag_both = both[0], both[1]
    else:
        real_both = jnp.einsum(form, real_part, joined, precision=highest)
        imag_both = jnp.einsum(form, imag_part, joined, precision=highest)
    real_cos = lax.slice_in_dim(real_both, 0, count, axis=axis)
    real_sin = lax.slice_in_dim(real_both, count, 2 * count, axis=axis)
    imag_cos = lax.slice_in_dim(imag_both, 0, count, axis=axis)
    imag_sin = lax.slice_in_dim(imag_both, count, 2 * count, axis=axis)
    if inverse:
        return (real_cos - imag_sin, imag_cos + real_sin)
    return (real_cos + imag_sin, imag_cos - real_sin)


def twiddle_apply(real_part, imag_part, twiddle, inverse):
    twiddle_cos, twiddle_sin = twiddle
    if inverse:
        return (
            real_part * twiddle_cos - imag_part * twiddle_sin,
            imag_part * twiddle_cos + real_part * twiddle_sin,
        )
    return (
        real_part * twiddle_cos + imag_part * twiddle_sin,
        imag_part * twiddle_cos - real_part * twiddle_sin,
    )


def along_last(values, plan, inverse, split=False, split_in=False):
    outer_tables, inner_tables, twiddle = plan
    outer_len = outer_tables[0].shape[0]
    inner_len = inner_tables[0].shape[0]
    if split_in:
        real_part = values[..., 0, :, :, :]
        imag_part = values[..., 1, :, :, :]
        shape = real_part.shape[:-2] + (outer_len * inner_len,)
    else:
        real_part = values[..., 0, :, :]
        imag_part = values[..., 1, :, :]
        shape = real_part.shape
    length = shape[-1]
    real_part = real_part.reshape(shape[:-1] + (outer_len, inner_len))
    imag_part = imag_part.reshape(shape[:-1] + (outer_len, inner_len))
    outer_form = "...ab,ak->...kb"
    inner_form = "...ab,bl->...al"
    if inverse:
        real_part, imag_part = complex_contract(
            real_part, imag_part, inner_tables, inner_form, True
        )
        real_part, imag_part = twiddle_apply(real_part, imag_part, twiddle, True)
        real_part, imag_part = complex_contract(
            real_part, imag_part, outer_tables, outer_form, True
        )
    else:
        real_part, imag_part = complex_contract(
            real_part, imag_part, outer_tables, outer_form, False
        )
        real_part, imag_part = twiddle_apply(real_part, imag_part, twiddle, False)
        real_part, imag_part = complex_contract(
            real_part, imag_part, inner_tables, inner_form, False
        )
    if split:
        result = jnp.stack([real_part, imag_part], axis=-4)
    else:
        result = jnp.stack([real_part.reshape(shape), imag_part.reshape(shape)], axis=-3)
    if inverse:
        return result * (1.0 / length)
    return result


def along_first(values, plan, inverse):
    outer_tables, inner_tables, twiddle = plan
    outer_len = outer_tables[0].shape[0]
    inner_len = inner_tables[0].shape[0]
    real_part = values[..., 0, :, :]
    imag_part = values[..., 1, :, :]
    shape = real_part.shape
    length = shape[-2]
    split_shape = shape[:-2] + (outer_len, inner_len, shape[-1])
    real_part = real_part.reshape(split_shape)
    imag_part = imag_part.reshape(split_shape)
    twiddle_cols = (twiddle[0][:, :, None], twiddle[1][:, :, None])
    outer_form = "...abw,ak->...kbw"
    inner_form = "...abw,bl->...alw"
    if inverse:
        real_part, imag_part = complex_contract(
            real_part, imag_part, inner_tables, inner_form, True
        )
        real_part, imag_part = twiddle_apply(real_part, imag_part, twiddle_cols, True)
        real_part, imag_part = complex_contract(
            real_part, imag_part, outer_tables, outer_form, True
        )
    else:
        real_part, imag_part = complex_contract(
            real_part, imag_part, outer_tables, outer_form, False
        )
        real_part, imag_part = twiddle_apply(real_part, imag_part, twiddle_cols, False)
        real_part, imag_part = complex_contract(
            real_part, imag_part, inner_tables, inner_form, False
        )
    result = jnp.stack([real_part.reshape(shape), imag_part.reshape(shape)], axis=-3)
    if inverse:
        return result * (1.0 / length)
    return result


def rows_to_columns(values, slabs, width):
    lead = values.shape[:-3]
    rank = len(lead)
    rows = values.shape[-2]
    parts = values.shape[-3]
    blocks = values.reshape(lead + (parts, rows, slabs, width))
    order = (rank, rank + 2, rank + 1) + tuple(range(rank)) + (rank + 3,)
    lanes = width
    for size in lead:
        lanes *= size
    outgoing = jnp.transpose(blocks, order).reshape(parts, slabs, rows, lanes)
    incoming = lax.all_to_all(outgoing, "slab", split_axis=1, concat_axis=1, tiled=True)
    incoming = incoming.reshape(parts, slabs * rows, lanes)
    return tuple(incoming[part] for part in range(parts))


def columns_to_rows(real_part, imag_part, slabs, width, count):
    length = real_part.shape[0]
    rows = length // slabs
    outgoing = jnp.stack([real_part, imag_part]).reshape(2, slabs, rows, count * width)
    incoming = lax.all_to_all(outgoing, "slab", split_axis=1, concat_axis=1, tiled=True)
    incoming = incoming.reshape(2, slabs, rows, count, width)
    return jnp.transpose(incoming, (3, 0, 2, 1, 4)).reshape(count, 2, rows, slabs * width)


def along_columns(real_part, imag_part, plan, inverse):
    outer_tables, inner_tables, twiddle = plan
    outer_len = outer_tables[0].shape[0]
    inner_len = inner_tables[0].shape[0]
    length, lanes = real_part.shape

    def contract(tables, real_in, imag_in, axis):
        joined = jnp.concatenate(tables, axis=1)
        count = tables[0].shape[1]
        stacked_dims = (((0,), (axis + 1,)), ((), ()))
        both = lax.dot_general(
            joined, jnp.stack([real_in, imag_in]), stacked_dims, precision=highest
        )
        real_both, imag_both = both[:, 0], both[:, 1]
        real_cos, real_sin = real_both[:count], real_both[count:]
        imag_cos, imag_sin = imag_both[:count], imag_both[count:]
        if inverse:
            return (real_cos - imag_sin, imag_cos + real_sin)
        return (real_cos + imag_sin, imag_cos - real_sin)

    if inverse:
        real_in = real_part.reshape(inner_len, outer_len, lanes)
        imag_in = imag_part.reshape(inner_len, outer_len, lanes)
        real_mid, imag_mid = contract(inner_tables, real_in, imag_in, 0)
        turn = (twiddle[0].T[:, :, None], twiddle[1].T[:, :, None])
        real_mid, imag_mid = twiddle_apply(real_mid, imag_mid, turn, True)
        real_out, imag_out = contract(outer_tables, real_mid, imag_mid, 1)
        scale = 1.0 / length
        return (real_out.reshape(length, lanes) * scale, imag_out.reshape(length, lanes) * scale)
    real_in = real_part.reshape(outer_len, inner_len, lanes)
    imag_in = imag_part.reshape(outer_len, inner_len, lanes)
    real_mid, imag_mid = contract(outer_tables, real_in, imag_in, 0)
    turn = (twiddle[0][:, :, None], twiddle[1][:, :, None])
    real_mid, imag_mid = twiddle_apply(real_mid, imag_mid, turn, False)
    real_out, imag_out = contract(inner_tables, real_mid, imag_mid, 1)
    return (real_out.reshape(length, lanes), imag_out.reshape(length, lanes))

def regroup_to_columns(values, width):
    depth, parts, rows, chunks, inner = values.shape
    per = inner // width
    lanes = depth * width
    inner_index = jnp.arange(inner, dtype=jnp.int32)
    out_index = jnp.arange(per * lanes, dtype=jnp.int32)
    out_group = out_index // lanes
    out_depth = (out_index // width) % depth
    out_cell = out_group * width + out_index % width
    depth_index = jnp.arange(depth, dtype=jnp.int32)
    permutation = (
        (depth_index[:, None, None] == out_depth[None, None, :])
        & (inner_index[None, :, None] == out_cell[None, None, :])
    ).astype(jnp.float32)
    moved = lax.dot_general(
        values, permutation, (((0, 4), (0, 1)), ((), ())), precision=highest
    )
    moved = moved.reshape(parts, rows, chunks, per, lanes)
    return jnp.transpose(moved, (2, 3, 0, 1, 4)).reshape(chunks * per, parts, rows, lanes)


def regroup_to_rows(real_part, imag_part, slabs, width, count):
    length, lanes = real_part.shape
    rows = length // slabs
    inner = 128
    per = inner // width
    chunks = slabs // per
    outgoing = jnp.transpose(
        jnp.stack([real_part, imag_part]).reshape(2, slabs, rows, lanes), (1, 0, 2, 3)
    )
    incoming = lax.all_to_all(outgoing, "slab", split_axis=0, concat_axis=0, tiled=True)
    incoming = incoming.reshape(chunks, per, 2, rows, lanes)
    lane_index = jnp.arange(lanes, dtype=jnp.int32)
    out_index = jnp.arange(count * inner, dtype=jnp.int32)
    out_depth = out_index // inner
    out_group = (out_index % inner) // width
    out_cell = out_index % width
    group_index = jnp.arange(per, dtype=jnp.int32)
    permutation = (
        (group_index[:, None, None] == out_group[None, None, :])
        & ((lane_index // width)[None, :, None] == out_depth[None, None, :])
        & ((lane_index % width)[None, :, None] == out_cell[None, None, :])
    ).astype(jnp.float32)
    moved = lax.dot_general(
        incoming, permutation, (((1, 4), (0, 1)), ((), ())), precision=highest
    )
    moved = moved.reshape(chunks, 2, rows, count, inner)
    return jnp.transpose(moved, (3, 1, 2, 0, 4))


def shards(volume, consensus, scaled_dual, amplitude, fresnel, ray_index, ray_weight):
    slice_cells = volume.shape[2]
    length = amplitude.shape[3]
    slabs = lax.axis_size("slab")
    width = length // slabs
    groups = lax.axis_size("group")
    inner_len = min(128, length)
    outer_len = length // inner_len
    outer_index = jnp.arange(outer_len, dtype=jnp.int32)
    inner_index = jnp.arange(inner_len, dtype=jnp.int32)
    twiddle_angle = (
        2.0 * math.pi / length * (outer_index[:, None] * inner_index[None, :]).astype(jnp.float32)
    )
    plan = (
        dft_tables(outer_len),
        dft_tables(inner_len),
        (jnp.cos(twiddle_angle), jnp.sin(twiddle_angle)),
    )
    cell_ids = jnp.arange(slice_cells, dtype=jnp.int32)
    projector = jnp.zeros((length, slice_cells), jnp.float32)
    for tap_number in range(ray_index.shape[1]):
        hit = (ray_index[0, tap_number][:, None] == cell_ids[None, :]).astype(jnp.float32)
        projector = projector + ray_weight[0, tap_number][:, None] * hit
    thickness = lax.dot_general(volume[0], projector, (((1,), (1,)), ((), ())), precision=highest)
    wavefront = jnp.stack([jnp.cos(thickness), jnp.sin(thickness)])
    row_spectrum = along_last(wavefront, plan, False)
    position = jnp.arange(length, dtype=jnp.int32)
    row_freq = position // inner_len + outer_len * (position % inner_len)
    centered_u = jnp.where(row_freq < length // 2, row_freq, row_freq - length)
    phase_u = (
        -math.pi * fresnel[:, None] * (centered_u * centered_u).astype(jnp.float32)[None, :]
        / HOLOGRAM
    )
    row_kernel_real = jnp.cos(phase_u)[:, None, :]
    row_kernel_imag = jnp.sin(phase_u)[:, None, :]
    u_fields = along_last(
        jnp.stack(
            [
                row_kernel_real * row_spectrum[0] - row_kernel_imag * row_spectrum[1],
                row_kernel_real * row_spectrum[1] + row_kernel_imag * row_spectrum[0],
            ],
            axis=1,
        ),
        plan,
        True,
        split=True,
    )
    measured = amplitude[0].reshape((DISTANCES, 1, amplitude.shape[2]) + u_fields.shape[-2:])
    packed = jnp.concatenate(
        [regroup_to_columns(u_fields, width), regroup_to_columns(measured, width)], axis=1
    )
    incoming = lax.all_to_all(packed, "slab", split_axis=0, concat_axis=0, tiled=True)
    column_real, column_imag, column_amplitude = (
        incoming[:, part].reshape(length, DISTANCES * width) for part in range(3)
    )
    centered_z = jnp.where(position < length // 2, position, position - length)
    phase_z = (
        -math.pi * fresnel[None, :, None]
        * (centered_z * centered_z).astype(jnp.float32)[:, None, None]
        / HOLOGRAM
    )
    lanes = DISTANCES * width
    phase_z = jnp.broadcast_to(phase_z, (length, DISTANCES, width)).reshape(length, lanes)
    kernel_real = jnp.cos(phase_z)
    kernel_imag = jnp.sin(phase_z)
    spectrum_real, spectrum_imag = along_columns(column_real, column_imag, plan, False)
    field_real, field_imag = along_columns(
        kernel_real * spectrum_real - kernel_imag * spectrum_imag,
        kernel_real * spectrum_imag + kernel_imag * spectrum_real,
        plan,
        True,
    )
    magnitude = jnp.sqrt(field_real * field_real + field_imag * field_imag)
    factor = column_amplitude / jnp.maximum(magnitude, mod_floor)
    moduli_real, moduli_imag = along_columns(field_real * factor, field_imag * factor, plan, False)
    turned_real, turned_imag = along_columns(
        kernel_real * moduli_real + kernel_imag * moduli_imag,
        kernel_real * moduli_imag - kernel_imag * moduli_real,
        plan,
        True,
    )
    row_moduli = along_last(
        regroup_to_rows(turned_real, turned_imag, slabs, width, DISTANCES),
        plan,
        False,
        split_in=True,
    )
    total_real = jnp.sum(
        row_kernel_real * row_moduli[:, 0] + row_kernel_imag * row_moduli[:, 1],
        axis=0,
    )
    total_imag = jnp.sum(
        row_kernel_real * row_moduli[:, 1] - row_kernel_imag * row_moduli[:, 0],
        axis=0,
    )
    back = along_last(jnp.stack([total_real, total_imag]) / DISTANCES, plan, True)
    gradient = jnp.cos(thickness) * back[1] - jnp.sin(thickness) * back[0]
    bprojected = jnp.matmul(gradient, projector, precision=highest)
    volume_next = volume[0] + step_size * (
        bprojected - penalty * (volume[0] - consensus + scaled_dual[0])
    )
    combined = volume_next + scaled_dual[0]
    total = combined
    step = 1
    while step < groups:
        pairs = [(index, index ^ step) for index in range(groups)]
        total = total + lax.ppermute(total, "group", pairs)
        step *= 2
    consensus_next = total / groups
    dual_next = scaled_dual[0] + volume_next - consensus_next
    return (volume_next[None], consensus_next, dual_next[None])


def solution(mesh):
    placed = (
        P("group", "slab", None),
        P("slab", None),
        P("group", "slab", None),
        P("group", None, "slab", None),
        P(),
        P("group", None, None),
        P("group", None, None),
    )
    return jax.shard_map(
        shards,
        mesh=mesh,
        in_specs=placed,
        out_specs=(P("group", "slab", None), P("slab", None), P("group", "slab", None)),
        check_vma=False,
    )
```

```python
import math

import jax
import jax.numpy as jnp
from jax import lax
from jax.sharding import PartitionSpec as P

HOLOGRAM = 1024
DISTANCES = 4


step_size = 0.5
penalty = 0.5
mod_floor = 0.25
highest = lax.Precision.HIGHEST


def dft_tables(count):
    index = jnp.arange(count, dtype=jnp.int32)
    angle = 2.0 * math.pi / count * (index[:, None] * index[None, :] % count).astype(jnp.float32)
    return (jnp.cos(angle), jnp.sin(angle))


def complex_contract(real_part, imag_part, tables, form, inverse):
    joined = jnp.concatenate(tables, axis=1)
    count = tables[0].shape[1]
    out_spec = form.split("->")[1]
    axis = out_spec.index(form.split(",")[1][1]) - len(out_spec)
    if axis == -2:
        both = jnp.einsum(form, jnp.stack([real_part, imag_part]), joined, precision=highest)
        real_both, imag_both = both[0], both[1]
    else:
        real_both = jnp.einsum(form, real_part, joined, precision=highest)
        imag_both = jnp.einsum(form, imag_part, joined, precision=highest)
    real_cos = lax.slice_in_dim(real_both, 0, count, axis=axis)
    real_sin = lax.slice_in_dim(real_both, count, 2 * count, axis=axis)
    imag_cos = lax.slice_in_dim(imag_both, 0, count, axis=axis)
    imag_sin = lax.slice_in_dim(imag_both, count, 2 * count, axis=axis)
    if inverse:
        return (real_cos - imag_sin, imag_cos + real_sin)
    return (real_cos + imag_sin, imag_cos - real_sin)


def twiddle_apply(real_part, imag_part, twiddle, inverse):
    twiddle_cos, twiddle_sin = twiddle
    if inverse:
        return (
            real_part * twiddle_cos - imag_part * twiddle_sin,
            imag_part * twiddle_cos + real_part * twiddle_sin,
        )
    return (
        real_part * twiddle_cos + imag_part * twiddle_sin,
        imag_part * twiddle_cos - real_part * twiddle_sin,
    )


def along_last(values, plan, inverse, split=False, split_in=False):
    outer_tables, inner_tables, twiddle = plan
    outer_len = outer_tables[0].shape[0]
    inner_len = inner_tables[0].shape[0]
    if split_in:
        real_part = values[..., 0, :, :, :]
        imag_part = values[..., 1, :, :, :]
        shape = real_part.shape[:-2] + (outer_len * inner_len,)
    else:
        real_part = values[..., 0, :, :]
        imag_part = values[..., 1, :, :]
        shape = real_part.shape
    length = shape[-1]
    real_part = real_part.reshape(shape[:-1] + (outer_len, inner_len))
    imag_part = imag_part.reshape(shape[:-1] + (outer_len, inner_len))
    outer_form = "...ab,ak->...kb"
    inner_form = "...ab,bl->...al"
    if inverse:
        real_part, imag_part = complex_contract(
            real_part, imag_part, inner_tables, inner_form, True
        )
        real_part, imag_part = twiddle_apply(real_part, imag_part, twiddle, True)
        real_part, imag_part = complex_contract(
            real_part, imag_part, outer_tables, outer_form, True
        )
    else:
        real_part, imag_part = complex_contract(
            real_part, imag_part, outer_tables, outer_form, False
        )
        real_part, imag_part = twiddle_apply(real_part, imag_part, twiddle, False)
        real_part, imag_part = complex_contract(
            real_part, imag_part, inner_tables, inner_form, False
        )
    if split:
        result = jnp.stack([real_part, imag_part], axis=-4)
    else:
        result = jnp.stack([real_part.reshape(shape), imag_part.reshape(shape)], axis=-3)
    if inverse:
        return result * (1.0 / length)
    return result


def along_first(values, plan, inverse):
    outer_tables, inner_tables, twiddle = plan
    outer_len = outer_tables[0].shape[0]
    inner_len = inner_tables[0].shape[0]
    real_part = values[..., 0, :, :]
    imag_part = values[..., 1, :, :]
    shape = real_part.shape
    length = shape[-2]
    split_shape = shape[:-2] + (outer_len, inner_len, shape[-1])
    real_part = real_part.reshape(split_shape)
    imag_part = imag_part.reshape(split_shape)
    twiddle_cols = (twiddle[0][:, :, None], twiddle[1][:, :, None])
    outer_form = "...abw,ak->...kbw"
    inner_form = "...abw,bl->...alw"
    if inverse:
        real_part, imag_part = complex_contract(
            real_part, imag_part, inner_tables, inner_form, True
        )
        real_part, imag_part = twiddle_apply(real_part, imag_part, twiddle_cols, True)
        real_part, imag_part = complex_contract(
            real_part, imag_part, outer_tables, outer_form, True
        )
    else:
        real_part, imag_part = complex_contract(
            real_part, imag_part, outer_tables, outer_form, False
        )
        real_part, imag_part = twiddle_apply(real_part, imag_part, twiddle_cols, False)
        real_part, imag_part = complex_contract(
            real_part, imag_part, inner_tables, inner_form, False
        )
    result = jnp.stack([real_part.reshape(shape), imag_part.reshape(shape)], axis=-3)
    if inverse:
        return result * (1.0 / length)
    return result


def rows_to_columns(values, slabs, width):
    lead = values.shape[:-3]
    rank = len(lead)
    rows = values.shape[-2]
    parts = values.shape[-3]
    blocks = values.reshape(lead + (parts, rows, slabs, width))
    order = (rank, rank + 2, rank + 1) + tuple(range(rank)) + (rank + 3,)
    lanes = width
    for size in lead:
        lanes *= size
    outgoing = jnp.transpose(blocks, order).reshape(parts, slabs, rows, lanes)
    incoming = lax.all_to_all(outgoing, "slab", split_axis=1, concat_axis=1, tiled=True)
    incoming = incoming.reshape(parts, slabs * rows, lanes)
    return tuple(incoming[part] for part in range(parts))


def columns_to_rows(real_part, imag_part, slabs, width, count):
    length = real_part.shape[0]
    rows = length // slabs
    outgoing = jnp.stack([real_part, imag_part]).reshape(2, slabs, rows, count * width)
    incoming = lax.all_to_all(outgoing, "slab", split_axis=1, concat_axis=1, tiled=True)
    incoming = incoming.reshape(2, slabs, rows, count, width)
    return jnp.transpose(incoming, (3, 0, 2, 1, 4)).reshape(count, 2, rows, slabs * width)


def along_columns(real_part, imag_part, plan, inverse):
    outer_tables, inner_tables, twiddle = plan
    outer_len = outer_tables[0].shape[0]
    inner_len = inner_tables[0].shape[0]
    length, lanes = real_part.shape

    def contract(tables, real_in, imag_in, axis):
        joined = jnp.concatenate(tables, axis=1)
        count = tables[0].shape[1]
        stacked_dims = (((0,), (axis + 1,)), ((), ()))
        both = lax.dot_general(
            joined, jnp.stack([real_in, imag_in]), stacked_dims, precision=highest
        )
        real_both, imag_both = both[:, 0], both[:, 1]
        real_cos, real_sin = real_both[:count], real_both[count:]
        imag_cos, imag_sin = imag_both[:count], imag_both[count:]
        if inverse:
            return (real_cos - imag_sin, imag_cos + real_sin)
        return (real_cos + imag_sin, imag_cos - real_sin)

    if inverse:
        real_in = real_part.reshape(inner_len, outer_len, lanes)
        imag_in = imag_part.reshape(inner_len, outer_len, lanes)
        real_mid, imag_mid = contract(inner_tables, real_in, imag_in, 0)
        turn = (twiddle[0].T[:, :, None], twiddle[1].T[:, :, None])
        real_mid, imag_mid = twiddle_apply(real_mid, imag_mid, turn, True)
        real_out, imag_out = contract(outer_tables, real_mid, imag_mid, 1)
        scale = 1.0 / length
        return (real_out.reshape(length, lanes) * scale, imag_out.reshape(length, lanes) * scale)
    real_in = real_part.reshape(outer_len, inner_len, lanes)
    imag_in = imag_part.reshape(outer_len, inner_len, lanes)
    real_mid, imag_mid = contract(outer_tables, real_in, imag_in, 0)
    turn = (twiddle[0][:, :, None], twiddle[1][:, :, None])
    real_mid, imag_mid = twiddle_apply(real_mid, imag_mid, turn, False)
    real_out, imag_out = contract(inner_tables, real_mid, imag_mid, 1)
    return (real_out.reshape(length, lanes), imag_out.reshape(length, lanes))

def regroup_to_columns(values, width):
    depth, parts, rows, chunks, inner = values.shape
    per = inner // width
    lanes = depth * width
    inner_index = jnp.arange(inner, dtype=jnp.int32)
    out_index = jnp.arange(per * lanes, dtype=jnp.int32)
    out_group = out_index // lanes
    out_depth = (out_index // width) % depth
    out_cell = out_group * width + out_index % width
    depth_index = jnp.arange(depth, dtype=jnp.int32)
    permutation = (
        (depth_index[:, None, None] == out_depth[None, None, :])
        & (inner_index[None, :, None] == out_cell[None, None, :])
    ).astype(jnp.float32)
    moved = lax.dot_general(
        values, permutation, (((0, 4), (0, 1)), ((), ())), precision=highest
    )
    moved = moved.reshape(parts, rows, chunks, per, lanes)
    return jnp.transpose(moved, (2, 3, 0, 1, 4)).reshape(chunks * per, parts, rows, lanes)


def regroup_to_rows(real_part, imag_part, slabs, width, count):
    length, lanes = real_part.shape
    rows = length // slabs
    inner = 128
    per = inner // width
    chunks = slabs // per
    outgoing = jnp.transpose(
        jnp.stack([real_part, imag_part]).reshape(2, slabs, rows, lanes), (1, 0, 2, 3)
    )
    incoming = lax.all_to_all(outgoing, "slab", split_axis=0, concat_axis=0, tiled=True)
    incoming = incoming.reshape(chunks, per, 2, rows, lanes)
    lane_index = jnp.arange(lanes, dtype=jnp.int32)
    out_index = jnp.arange(count * inner, dtype=jnp.int32)
    out_depth = out_index // inner
    out_group = (out_index % inner) // width
    out_cell = out_index % width
    group_index = jnp.arange(per, dtype=jnp.int32)
    permutation = (
        (group_index[:, None, None] == out_group[None, None, :])
        & ((lane_index // width)[None, :, None] == out_depth[None, None, :])
        & ((lane_index % width)[None, :, None] == out_cell[None, None, :])
    ).astype(jnp.float32)
    moved = lax.dot_general(
        incoming, permutation, (((1, 4), (0, 1)), ((), ())), precision=highest
    )
    moved = moved.reshape(chunks, 2, rows, count, inner)
    return jnp.transpose(moved, (3, 1, 2, 0, 4))


def shards(volume, consensus, scaled_dual, amplitude, fresnel, ray_index, ray_weight):
    slice_cells = volume.shape[2]
    length = amplitude.shape[3]
    slabs = lax.axis_size("slab")
    width = length // slabs
    groups = lax.axis_size("group")
    inner_len = min(128, length)
    outer_len = length // inner_len
    outer_index = jnp.arange(outer_len, dtype=jnp.int32)
    inner_index = jnp.arange(inner_len, dtype=jnp.int32)
    twiddle_angle = (
        2.0 * math.pi / length * (outer_index[:, None] * inner_index[None, :]).astype(jnp.float32)
    )
    plan = (
        dft_tables(outer_len),
        dft_tables(inner_len),
        (jnp.cos(twiddle_angle), jnp.sin(twiddle_angle)),
    )
    cell_ids = jnp.arange(slice_cells, dtype=jnp.int32)
    projector = jnp.zeros((length, slice_cells), jnp.float32)
    for tap_number in range(ray_index.shape[1]):
        hit = (ray_index[0, tap_number][:, None] == cell_ids[None, :]).astype(jnp.float32)
        projector = projector + ray_weight[0, tap_number][:, None] * hit
    thickness = lax.dot_general(volume[0], projector, (((1,), (1,)), ((), ())), precision=highest)
    wavefront = jnp.stack([jnp.cos(thickness), jnp.sin(thickness)])
    row_spectrum = along_last(wavefront, plan, False)
    position = jnp.arange(length, dtype=jnp.int32)
    row_freq = position // inner_len + outer_len * (position % inner_len)
    centered_u = jnp.where(row_freq < length // 2, row_freq, row_freq - length)
    phase_u = (
        -math.pi * fresnel[:, None] * (centered_u * centered_u).astype(jnp.float32)[None, :]
        / HOLOGRAM
    )
    row_kernel_real = jnp.cos(phase_u)[:, None, :]
    row_kernel_imag = jnp.sin(phase_u)[:, None, :]
    u_fields = along_last(
        jnp.stack(
            [
                row_kernel_real * row_spectrum[0] - row_kernel_imag * row_spectrum[1],
                row_kernel_real * row_spectrum[1] + row_kernel_imag * row_spectrum[0],
            ],
            axis=1,
        ),
        plan,
        True,
        split=True,
    )
    measured = amplitude[0].reshape((DISTANCES, 1, amplitude.shape[2]) + u_fields.shape[-2:])
    packed = jnp.concatenate(
        [regroup_to_columns(u_fields, width), regroup_to_columns(measured, width)], axis=1
    )
    incoming = lax.all_to_all(packed, "slab", split_axis=0, concat_axis=0, tiled=True)
    column_real, column_imag, column_amplitude = (
        incoming[:, part].reshape(length, DISTANCES * width) for part in range(3)
    )
    centered_z = jnp.where(position < length // 2, position, position - length)
    phase_z = (
        -math.pi * fresnel[None, :, None]
        * (centered_z * centered_z).astype(jnp.float32)[:, None, None]
        / HOLOGRAM
    )
    lanes = DISTANCES * width
    phase_z = jnp.broadcast_to(phase_z, (length, DISTANCES, width)).reshape(length, lanes)
    kernel_real = jnp.cos(phase_z)
    kernel_imag = jnp.sin(phase_z)
    spectrum_real, spectrum_imag = along_columns(column_real, column_imag, plan, False)
    field_real, field_imag = along_columns(
        kernel_real * spectrum_real - kernel_imag * spectrum_imag,
        kernel_real * spectrum_imag + kernel_imag * spectrum_real,
        plan,
        True,
    )
    magnitude = jnp.sqrt(field_real * field_real + field_imag * field_imag)
    factor = column_amplitude / jnp.maximum(magnitude, mod_floor)
    moduli_real, moduli_imag = along_columns(field_real * factor, field_imag * factor, plan, False)
    turned_real, turned_imag = along_columns(
        kernel_real * moduli_real + kernel_imag * moduli_imag,
        kernel_real * moduli_imag - kernel_imag * moduli_real,
        plan,
        True,
    )
    row_moduli = along_last(
        regroup_to_rows(turned_real, turned_imag, slabs, width, DISTANCES),
        plan,
        False,
        split_in=True,
    )
    total_real = jnp.sum(
        row_kernel_real * row_moduli[:, 0] + row_kernel_imag * row_moduli[:, 1],
        axis=0,
    )
    total_imag = jnp.sum(
        row_kernel_real * row_moduli[:, 1] - row_kernel_imag * row_moduli[:, 0],
        axis=0,
    )
    back = along_last(jnp.stack([total_real, total_imag]) / DISTANCES, plan, True)
    gradient = jnp.cos(thickness) * back[1] - jnp.sin(thickness) * back[0]
    bprojected = jnp.matmul(gradient, projector, precision=highest)
    volume_next = volume[0] + step_size * (
        bprojected - penalty * (volume[0] - consensus + scaled_dual[0])
    )
    combined = volume_next + scaled_dual[0]
    total = combined
    step = 1
    while step < groups:
        pairs = [(index, index ^ step) for index in range(groups)]
        total = total + lax.ppermute(total, "group", pairs)
        step *= 2
    consensus_next = total / groups
    dual_next = scaled_dual[0] + volume_next - consensus_next
    return (volume_next[None], consensus_next, dual_next[None])


def solution(mesh):
    placed = (
        P("group", "slab", None),
        P("slab", None),
        P("group", "slab", None),
        P("group", None, "slab", None),
        P(),
        P("group", None, None),
        P("group", None, None),
    )
    return jax.shard_map(
        shards,
        mesh=mesh,
        in_specs=placed,
        out_specs=(P("group", "slab", None), P("slab", None), P("group", "slab", None)),
        check_vma=False,
    )
```

```python
import math

import jax
import jax.numpy as jnp
from jax import lax
from jax.sharding import PartitionSpec as P

HOLOGRAM = 1024
DISTANCES = 4


step_size = 0.5
penalty = 0.5
mod_floor = 0.25
highest = lax.Precision.HIGHEST


def dft_tables(count):
    index = jnp.arange(count, dtype=jnp.int32)
    angle = 2.0 * math.pi / count * (index[:, None] * index[None, :] % count).astype(jnp.float32)
    return (jnp.cos(angle), jnp.sin(angle))


def complex_contract(real_part, imag_part, tables, form, inverse):
    joined = jnp.concatenate(tables, axis=1)
    count = tables[0].shape[1]
    out_spec = form.split("->")[1]
    axis = out_spec.index(form.split(",")[1][1]) - len(out_spec)
    real_both = jnp.einsum(form, real_part, joined, precision=highest)
    imag_both = jnp.einsum(form, imag_part, joined, precision=highest)
    real_cos = lax.slice_in_dim(real_both, 0, count, axis=axis)
    real_sin = lax.slice_in_dim(real_both, count, 2 * count, axis=axis)
    imag_cos = lax.slice_in_dim(imag_both, 0, count, axis=axis)
    imag_sin = lax.slice_in_dim(imag_both, count, 2 * count, axis=axis)
    if inverse:
        return (real_cos - imag_sin, imag_cos + real_sin)
    return (real_cos + imag_sin, imag_cos - real_sin)


def twiddle_apply(real_part, imag_part, twiddle, inverse):
    twiddle_cos, twiddle_sin = twiddle
    if inverse:
        return (
            real_part * twiddle_cos - imag_part * twiddle_sin,
            imag_part * twiddle_cos + real_part * twiddle_sin,
        )
    return (
        real_part * twiddle_cos + imag_part * twiddle_sin,
        imag_part * twiddle_cos - real_part * twiddle_sin,
    )


def along_last(values, plan, inverse, split=False, split_in=False):
    outer_tables, inner_tables, twiddle = plan
    outer_len = outer_tables[0].shape[0]
    inner_len = inner_tables[0].shape[0]
    if split_in:
        real_part = values[..., 0, :, :, :]
        imag_part = values[..., 1, :, :, :]
        shape = real_part.shape[:-2] + (outer_len * inner_len,)
    else:
        real_part = values[..., 0, :, :]
        imag_part = values[..., 1, :, :]
        shape = real_part.shape
    length = shape[-1]
    real_part = real_part.reshape(shape[:-1] + (outer_len, inner_len))
    imag_part = imag_part.reshape(shape[:-1] + (outer_len, inner_len))
    outer_form = "...ab,ak->...kb"
    inner_form = "...ab,bl->...al"
    if inverse:
        real_part, imag_part = complex_contract(
            real_part, imag_part, inner_tables, inner_form, True
        )
        real_part, imag_part = twiddle_apply(real_part, imag_part, twiddle, True)
        real_part, imag_part = complex_contract(
            real_part, imag_part, outer_tables, outer_form, True
        )
    else:
        real_part, imag_part = complex_contract(
            real_part, imag_part, outer_tables, outer_form, False
        )
        real_part, imag_part = twiddle_apply(real_part, imag_part, twiddle, False)
        real_part, imag_part = complex_contract(
            real_part, imag_part, inner_tables, inner_form, False
        )
    if split:
        result = jnp.stack([real_part, imag_part], axis=-4)
    else:
        result = jnp.stack([real_part.reshape(shape), imag_part.reshape(shape)], axis=-3)
    if inverse:
        return result * (1.0 / length)
    return result


def along_first(values, plan, inverse):
    outer_tables, inner_tables, twiddle = plan
    outer_len = outer_tables[0].shape[0]
    inner_len = inner_tables[0].shape[0]
    real_part = values[..., 0, :, :]
    imag_part = values[..., 1, :, :]
    shape = real_part.shape
    length = shape[-2]
    split_shape = shape[:-2] + (outer_len, inner_len, shape[-1])
    real_part = real_part.reshape(split_shape)
    imag_part = imag_part.reshape(split_shape)
    twiddle_cols = (twiddle[0][:, :, None], twiddle[1][:, :, None])
    outer_form = "...abw,ak->...kbw"
    inner_form = "...abw,bl->...alw"
    if inverse:
        real_part, imag_part = complex_contract(
            real_part, imag_part, inner_tables, inner_form, True
        )
        real_part, imag_part = twiddle_apply(real_part, imag_part, twiddle_cols, True)
        real_part, imag_part = complex_contract(
            real_part, imag_part, outer_tables, outer_form, True
        )
    else:
        real_part, imag_part = complex_contract(
            real_part, imag_part, outer_tables, outer_form, False
        )
        real_part, imag_part = twiddle_apply(real_part, imag_part, twiddle_cols, False)
        real_part, imag_part = complex_contract(
            real_part, imag_part, inner_tables, inner_form, False
        )
    result = jnp.stack([real_part.reshape(shape), imag_part.reshape(shape)], axis=-3)
    if inverse:
        return result * (1.0 / length)
    return result


def rows_to_columns(values, slabs, width):
    lead = values.shape[:-3]
    rank = len(lead)
    rows = values.shape[-2]
    parts = values.shape[-3]
    blocks = values.reshape(lead + (parts, rows, slabs, width))
    order = (rank, rank + 2, rank + 1) + tuple(range(rank)) + (rank + 3,)
    lanes = width
    for size in lead:
        lanes *= size
    outgoing = jnp.transpose(blocks, order).reshape(parts, slabs, rows, lanes)
    incoming = lax.all_to_all(outgoing, "slab", split_axis=1, concat_axis=1, tiled=True)
    incoming = incoming.reshape(parts, slabs * rows, lanes)
    return tuple(incoming[part] for part in range(parts))


def columns_to_rows(real_part, imag_part, slabs, width, count):
    length = real_part.shape[0]
    rows = length // slabs
    outgoing = jnp.stack([real_part, imag_part]).reshape(2, slabs, rows, count * width)
    incoming = lax.all_to_all(outgoing, "slab", split_axis=1, concat_axis=1, tiled=True)
    incoming = incoming.reshape(2, slabs, rows, count, width)
    return jnp.transpose(incoming, (3, 0, 2, 1, 4)).reshape(count, 2, rows, slabs * width)


def along_columns(real_part, imag_part, plan, inverse):
    outer_tables, inner_tables, twiddle = plan
    outer_len = outer_tables[0].shape[0]
    inner_len = inner_tables[0].shape[0]
    length, lanes = real_part.shape

    def contract(tables, real_in, imag_in, axis):
        joined = jnp.concatenate(tables, axis=1)
        count = tables[0].shape[1]
        stacked_dims = (((0,), (axis + 1,)), ((), ()))
        both = lax.dot_general(
            joined, jnp.stack([real_in, imag_in]), stacked_dims, precision=highest
        )
        real_both, imag_both = both[:, 0], both[:, 1]
        real_cos, real_sin = real_both[:count], real_both[count:]
        imag_cos, imag_sin = imag_both[:count], imag_both[count:]
        if inverse:
            return (real_cos - imag_sin, imag_cos + real_sin)
        return (real_cos + imag_sin, imag_cos - real_sin)

    if inverse:
        real_in = real_part.reshape(inner_len, outer_len, lanes)
        imag_in = imag_part.reshape(inner_len, outer_len, lanes)
        real_mid, imag_mid = contract(inner_tables, real_in, imag_in, 0)
        turn = (twiddle[0].T[:, :, None], twiddle[1].T[:, :, None])
        real_mid, imag_mid = twiddle_apply(real_mid, imag_mid, turn, True)
        real_out, imag_out = contract(outer_tables, real_mid, imag_mid, 1)
        scale = 1.0 / length
        return (real_out.reshape(length, lanes) * scale, imag_out.reshape(length, lanes) * scale)
    real_in = real_part.reshape(outer_len, inner_len, lanes)
    imag_in = imag_part.reshape(outer_len, inner_len, lanes)
    real_mid, imag_mid = contract(outer_tables, real_in, imag_in, 0)
    turn = (twiddle[0][:, :, None], twiddle[1][:, :, None])
    real_mid, imag_mid = twiddle_apply(real_mid, imag_mid, turn, False)
    real_out, imag_out = contract(inner_tables, real_mid, imag_mid, 1)
    return (real_out.reshape(length, lanes), imag_out.reshape(length, lanes))

def regroup_to_columns(values, width):
    depth, parts, rows, chunks, inner = values.shape
    per = inner // width
    lanes = depth * width
    inner_index = jnp.arange(inner, dtype=jnp.int32)
    out_index = jnp.arange(per * lanes, dtype=jnp.int32)
    out_group = out_index // lanes
    out_depth = (out_index // width) % depth
    out_cell = out_group * width + out_index % width
    depth_index = jnp.arange(depth, dtype=jnp.int32)
    permutation = (
        (depth_index[:, None, None] == out_depth[None, None, :])
        & (inner_index[None, :, None] == out_cell[None, None, :])
    ).astype(jnp.float32)
    moved = lax.dot_general(
        values, permutation, (((0, 4), (0, 1)), ((), ())), precision=highest
    )
    moved = moved.reshape(parts, rows, chunks, per, lanes)
    return jnp.transpose(moved, (2, 3, 0, 1, 4)).reshape(chunks * per, parts, rows, lanes)


def regroup_to_rows(real_part, imag_part, slabs, width, count):
    length, lanes = real_part.shape
    rows = length // slabs
    inner = 128
    per = inner // width
    chunks = slabs // per
    outgoing = jnp.transpose(
        jnp.stack([real_part, imag_part]).reshape(2, slabs, rows, lanes), (1, 0, 2, 3)
    )
    incoming = lax.all_to_all(outgoing, "slab", split_axis=0, concat_axis=0, tiled=True)
    incoming = incoming.reshape(chunks, per, 2, rows, lanes)
    lane_index = jnp.arange(lanes, dtype=jnp.int32)
    out_index = jnp.arange(count * inner, dtype=jnp.int32)
    out_depth = out_index // inner
    out_group = (out_index % inner) // width
    out_cell = out_index % width
    group_index = jnp.arange(per, dtype=jnp.int32)
    permutation = (
        (group_index[:, None, None] == out_group[None, None, :])
        & ((lane_index // width)[None, :, None] == out_depth[None, None, :])
        & ((lane_index % width)[None, :, None] == out_cell[None, None, :])
    ).astype(jnp.float32)
    moved = lax.dot_general(
        incoming, permutation, (((1, 4), (0, 1)), ((), ())), precision=highest
    )
    moved = moved.reshape(chunks, 2, rows, count, inner)
    return jnp.transpose(moved, (3, 1, 2, 0, 4))


def shards(volume, consensus, scaled_dual, amplitude, fresnel, ray_index, ray_weight):
    slice_cells = volume.shape[2]
    length = amplitude.shape[3]
    slabs = lax.axis_size("slab")
    width = length // slabs
    groups = lax.axis_size("group")
    inner_len = min(128, length)
    outer_len = length // inner_len
    outer_index = jnp.arange(outer_len, dtype=jnp.int32)
    inner_index = jnp.arange(inner_len, dtype=jnp.int32)
    twiddle_angle = (
        2.0 * math.pi / length * (outer_index[:, None] * inner_index[None, :]).astype(jnp.float32)
    )
    plan = (
        dft_tables(outer_len),
        dft_tables(inner_len),
        (jnp.cos(twiddle_angle), jnp.sin(twiddle_angle)),
    )
    cell_ids = jnp.arange(slice_cells, dtype=jnp.int32)
    projector = jnp.zeros((length, slice_cells), jnp.float32)
    for tap_number in range(ray_index.shape[1]):
        hit = (ray_index[0, tap_number][:, None] == cell_ids[None, :]).astype(jnp.float32)
        projector = projector + ray_weight[0, tap_number][:, None] * hit
    thickness = lax.dot_general(volume[0], projector, (((1,), (1,)), ((), ())), precision=highest)
    wavefront = jnp.stack([jnp.cos(thickness), jnp.sin(thickness)])
    row_spectrum = along_last(wavefront, plan, False)
    position = jnp.arange(length, dtype=jnp.int32)
    row_freq = position // inner_len + outer_len * (position % inner_len)
    centered_u = jnp.where(row_freq < length // 2, row_freq, row_freq - length)
    phase_u = (
        -math.pi * fresnel[:, None] * (centered_u * centered_u).astype(jnp.float32)[None, :]
        / HOLOGRAM
    )
    row_kernel_real = jnp.cos(phase_u)[:, None, :]
    row_kernel_imag = jnp.sin(phase_u)[:, None, :]
    u_fields = along_last(
        jnp.stack(
            [
                row_kernel_real * row_spectrum[0] - row_kernel_imag * row_spectrum[1],
                row_kernel_real * row_spectrum[1] + row_kernel_imag * row_spectrum[0],
            ],
            axis=1,
        ),
        plan,
        True,
        split=True,
    )
    measured = amplitude[0].reshape((DISTANCES, 1, amplitude.shape[2]) + u_fields.shape[-2:])
    packed = jnp.concatenate(
        [regroup_to_columns(u_fields, width), regroup_to_columns(measured, width)], axis=1
    )
    incoming = lax.all_to_all(packed, "slab", split_axis=0, concat_axis=0, tiled=True)
    column_real, column_imag, column_amplitude = (
        incoming[:, part].reshape(length, DISTANCES * width) for part in range(3)
    )
    centered_z = jnp.where(position < length // 2, position, position - length)
    phase_z = (
        -math.pi * fresnel[None, :, None]
        * (centered_z * centered_z).astype(jnp.float32)[:, None, None]
        / HOLOGRAM
    )
    lanes = DISTANCES * width
    phase_z = jnp.broadcast_to(phase_z, (length, DISTANCES, width)).reshape(length, lanes)
    kernel_real = jnp.cos(phase_z)
    kernel_imag = jnp.sin(phase_z)
    spectrum_real, spectrum_imag = along_columns(column_real, column_imag, plan, False)
    field_real, field_imag = along_columns(
        kernel_real * spectrum_real - kernel_imag * spectrum_imag,
        kernel_real * spectrum_imag + kernel_imag * spectrum_real,
        plan,
        True,
    )
    magnitude = jnp.sqrt(field_real * field_real + field_imag * field_imag)
    factor = column_amplitude / jnp.maximum(magnitude, mod_floor)
    moduli_real, moduli_imag = along_columns(field_real * factor, field_imag * factor, plan, False)
    turned_real, turned_imag = along_columns(
        kernel_real * moduli_real + kernel_imag * moduli_imag,
        kernel_real * moduli_imag - kernel_imag * moduli_real,
        plan,
        True,
    )
    row_moduli = along_last(
        regroup_to_rows(turned_real, turned_imag, slabs, width, DISTANCES),
        plan,
        False,
        split_in=True,
    )
    total_real = jnp.sum(
        row_kernel_real * row_moduli[:, 0] + row_kernel_imag * row_moduli[:, 1],
        axis=0,
    )
    total_imag = jnp.sum(
        row_kernel_real * row_moduli[:, 1] - row_kernel_imag * row_moduli[:, 0],
        axis=0,
    )
    back = along_last(jnp.stack([total_real, total_imag]) / DISTANCES, plan, True)
    gradient = jnp.cos(thickness) * back[1] - jnp.sin(thickness) * back[0]
    bprojected = jnp.matmul(gradient, projector, precision=highest)
    volume_next = volume[0] + step_size * (
        bprojected - penalty * (volume[0] - consensus + scaled_dual[0])
    )
    combined = volume_next + scaled_dual[0]
    total = combined + lax.ppermute(
        combined, "group", [(index, index ^ 1) for index in range(groups)]
    )
    others = [
        lax.ppermute(total, "group", [(index, index ^ step) for index in range(groups)])
        for step in (2, 4, 6)
    ]
    total = (total + others[0]) + (others[1] + others[2])
    consensus_next = total / groups
    dual_next = scaled_dual[0] + volume_next - consensus_next
    return (volume_next[None], consensus_next, dual_next[None])


def solution(mesh):
    placed = (
        P("group", "slab", None),
        P("slab", None),
        P("group", "slab", None),
        P("group", None, "slab", None),
        P(),
        P("group", None, None),
        P("group", None, None),
    )
    return jax.shard_map(
        shards,
        mesh=mesh,
        in_specs=placed,
        out_specs=(P("group", "slab", None), P("slab", None), P("group", "slab", None)),
        check_vma=False,
    )
```
